256 devices in a mesh: facet: 8 (over y_lo, x), vis: 16 (over z, core), spec: 2 (over y_hi).
Axes of the slice: x: 4, y: 4 (y_hi: 2, y_lo: 2; y = y_hi * 2 + y_lo), z: 8, core: 2. Of those that a mesh axis runs over, the one named last changes fastest.
Arguments:
- image: float32 [1024, 8, 4096], P(('facet', 'vis'), 'spec'), may hold values from 0 to 1
- wavelet_dual: float32 [1024, 8, 4096], P(('facet', 'vis'), 'spec'), may hold values from -6 to 6
- weights: float32 [1024, 4096], P(('facet', 'vis')), may hold values from 0.3 to 3
- kernels: bfloat16 [8, 16, 2, 256, 128], P('facet', 'vis'), may hold values from -0.375 to 0.375
- vis_data: bfloat16 [8, 16, 8, 2, 16, 256, 128], P('facet', 'vis', 'spec'), may hold values from -6 to 6
- tile_list: int32 [8, 16, 16], P('facet', 'vis'), may hold values from 0 to 31, as said below
- tile_count: int32 [8, 16], P('facet', 'vis'), may hold values from 4 to 16, as said below
Outputs:
- image_next: float32 [1024, 8, 4096], P(('facet', 'vis'), 'spec')
- dual_next: float32 [1024, 8, 4096], P(('facet', 'vis'), 'spec')
The draws below stay inside these ranges and needn't reach their ends.
Inputs may be any that keep to these rules, and one draw needn't show every extreme that they name: `tile_list`: the 16 slots of a block name distinct tiles; slots from tile_count on are unused. `tile_count`: every draw has a block with 16 occupied slots and one with the fewest allowed.
All inputs are finite; a program needn't handle non-finite values.
Results may differ from the reference program's by a relative error of at most 0.017.
Values may be sent and summed in bfloat16 or wider, within the bound.
No kernel may reach another device: no remote copies, remote signals or barrier semaphores. Data moves between devices by JAX's collectives and lax.ppermute only.
A program may use at most 128 MiB of HBM per device.

```python
import math
import jax
import jax.numpy as jnp
from jax import lax

FW = 4096
MVIS = 256
NFAC = 8
NBLK = 16
FROWS = 128
ROWS = 1024
CH = 8
NT = 32
KMAX = 16


def one_order(one_key):
    return jax.random.permutation(one_key, NT)


def draw_tile_list(key, part):
    blocks_all = NFAC * NBLK
    keys = jax.random.split(key, blocks_all)
    orders = jax.vmap(one_order)(keys)
    return orders[:, :KMAX].reshape(NFAC, NBLK, KMAX).astype(jnp.int32)


def draw_tile_count(key, part):
    blocks_all = NFAC * NBLK
    fewest = max(1, KMAX // 4)
    spread = KMAX - fewest
    draw_one = jax.random.randint(jax.random.fold_in(key, 1), (blocks_all,), 0, spread + 1)
    draw_two = jax.random.randint(jax.random.fold_in(key, 2), (blocks_all,), 0, spread + 1)
    counts = fewest + jnp.minimum(draw_one, draw_two)
    where_most = jax.random.randint(jax.random.fold_in(key, 3), (), 0, blocks_all)
    counts = counts.at[where_most].set(KMAX)
    counts = counts.at[(where_most + 1) % blocks_all].set(fewest)
    return counts.reshape(NFAC, NBLK).astype(jnp.int32)


def level_of(rng, shape, cuts, least, high):
    def one(dim, parts):
        steps = jax.random.uniform(jax.random.fold_in(jax.random.fold_in(rng, 6), dim), (parts,), jnp.float32, least / len(cuts), high / len(cuts))
        return jnp.repeat(jnp.exp(steps), shape[dim] // parts).reshape((-1,) + (1,) * (len(shape) - dim - 1))

    level = one(*cuts[0])
    for cut in cuts[1:]:
        level = level * one(*cut)
    return level


def scatter_about(rng, extent, deviation, bound, cuts=(), kind=jnp.bfloat16):
    factor_of = level_of(rng, extent, cuts, -0.22, 0.18) if cuts else 1.0
    result = jax.random.normal(rng, extent, jnp.float32) * deviation * factor_of
    return jnp.minimum(jnp.maximum(result, -bound), bound).astype(kind)


def setup_inputs(seed: int = 0) -> dict:
    key_of = jax.random.split(jax.random.key(seed), 8)
    image = jnp.clip(1.0 * jax.random.uniform(key_of[0], (ROWS, CH, FW), jnp.float32) ** level_of(key_of[0], (ROWS, CH, FW), ((0, 128), (1, 2)), -0.2, 0.2), 0.0, 1.0)
    wavelet_dual = scatter_about(key_of[1], (ROWS, CH, FW), 1.0, 6.0, ((0, 128), (1, 2)), jnp.float32)
    weights = jnp.clip(jnp.exp(math.log(3.0) - 2.3025851 * jax.random.uniform(key_of[2], (ROWS, FW), jnp.float32) ** level_of(key_of[2], (ROWS, FW), ((0, 128),), -0.2, 0.2)), 0.3, 3.0)
    kernels = scatter_about(key_of[3], (NFAC, NBLK, 2, MVIS, FROWS), (2 * FROWS) ** -0.5, 0.375, ((0, 8), (1, 16)))
    vis_data = scatter_about(key_of[4], (NFAC, NBLK, CH, 2, KMAX, MVIS, 128), 1.0, 6.0, ((0, 8), (1, 16), (2, 2)))
    tile_list = draw_tile_list(jax.random.fold_in(key_of[7], 71), 0)
    tile_count = draw_tile_count(jax.random.fold_in(key_of[7], 71), 0)
    return {"image": image, "wavelet_dual": wavelet_dual, "weights": weights, "kernels": kernels, "vis_data": vis_data, "tile_list": tile_list, "tile_count": tile_count}


root_three = math.sqrt(3.0)
norm_factor = 4.0 * math.sqrt(2.0)
low_taps = [(1.0 + root_three) / norm_factor, (3.0 + root_three) / norm_factor, (3.0 - root_three) / norm_factor, (1.0 - root_three) / norm_factor]
high_taps = [low_taps[3], -low_taps[2], low_taps[1], -low_taps[0]]
primal_step = 0.2
dual_step = 0.5

def kernel_blocks(kernel_pair):
    real_k = kernel_pair[0]
    imag_k = kernel_pair[1]
    top_row = jnp.stack([real_k, -imag_k], axis=1)
    bottom_row = jnp.stack([imag_k, real_k], axis=1)
    return jnp.stack([top_row, bottom_row], axis=0)

def reference(image, wavelet_dual, weights, kernels, vis_data, tile_list, tile_count):
    unit_scale = 1.0 / math.sqrt(FW)
    spectrum = jnp.fft.fft(image, axis=-1)
    grid = jnp.stack([jnp.real(spectrum), jnp.imag(spectrum)], axis=2) * unit_scale
    grid = lax.optimization_barrier(grid.astype(jnp.bfloat16))
    grid = grid.reshape(NFAC, FROWS, CH, 2, NT, 128)
    columns = jnp.arange(NT, dtype=jnp.int32)
    slot_index = jnp.arange(KMAX, dtype=jnp.int32)

    def facet_sum(packed):
        facet_grid, facet_kernels, facet_data, facet_lists, facet_counts = packed
        grid_wide = facet_grid.astype(jnp.float32)

        def block_step(running, block_args):
            kernel_pair, block_data, block_list, block_count = block_args
            stacked = kernel_blocks(kernel_pair).astype(jnp.float32)
            one_hot = (block_list[:, None] == columns[None, :]).astype(jnp.float32)
            picked = jnp.einsum('rcitn,kt->rcikn', grid_wide, one_hot)
            predicted = jnp.einsum('omir,rcikn->cokmn', stacked, picked)
            live_slots = (slot_index < block_count)[None, None, :, None, None]
            residual = jnp.where(live_slots, predicted - block_data.astype(jnp.float32), 0.0).astype(jnp.bfloat16)
            residual = lax.optimization_barrier(residual)
            partial_tiles = jnp.einsum('omir,cokmn->rcikn', stacked, residual.astype(jnp.float32))
            partial_tiles = lax.optimization_barrier(partial_tiles.astype(jnp.bfloat16))
            placed = jnp.einsum('rcikn,kt->rcitn', partial_tiles.astype(jnp.float32), one_hot)
            return (running + placed, None)
        zero_grid = jnp.zeros((FROWS, CH, 2, NT, 128), jnp.float32)
        facet_total, ignored = lax.scan(block_step, zero_grid, (facet_kernels, facet_data, facet_lists, facet_counts))
        return facet_total
    grid_sums = lax.map(facet_sum, (grid, kernels, vis_data, tile_list, tile_count))
    grid_sums = grid_sums.reshape(ROWS, CH, 2, FW)
    inverse = jnp.fft.ifft(lax.complex(grid_sums[:, :, 0], grid_sums[:, :, 1]), axis=-1)
    gradient = jnp.real(inverse) * (FW * unit_scale)
    padded_dual = jnp.concatenate([jnp.zeros((3, CH, FW), wavelet_dual.dtype), wavelet_dual], axis=0)
    synthesized = jnp.zeros_like(wavelet_dual)
    for offset in range(4):
        synthesized = synthesized + high_taps[offset] * padded_dual[3 - offset:3 - offset + ROWS]
    image_next = jnp.maximum(image - primal_step * (gradient + synthesized), 0.0)
    extrap = 2.0 * image_next - image
    padded_next = jnp.concatenate([extrap, jnp.zeros((3, CH, FW), extrap.dtype)], axis=0)
    detail = jnp.zeros_like(extrap)
    for offset in range(4):
        detail = detail + high_taps[offset] * padded_next[offset:offset + ROWS]
    update = wavelet_dual + dual_step * detail
    energy = lax.optimization_barrier(jnp.sum(update * update, axis=1))
    dual_next = update * weights[:, None, :] / jnp.maximum(weights, jnp.sqrt(energy))[:, None, :]
    return (image_next, dual_next)
```

```python
import math

import jax
import jax.numpy as jnp
from jax import lax
from jax.sharding import PartitionSpec as P

root_three = math.sqrt(3.0)
norm_factor = 4.0 * math.sqrt(2.0)
low_taps = [
    (1.0 + root_three) / norm_factor,
    (3.0 + root_three) / norm_factor,
    (3.0 - root_three) / norm_factor,
    (1.0 - root_three) / norm_factor,
]
high_taps = [low_taps[3], -low_taps[2], low_taps[1], -low_taps[0]]
primal_step = 0.2
dual_step = 0.5
tile_width = 128
highest = lax.Precision.HIGHEST


def shifted(value, axis, steps):
    count = lax.axis_size(axis)
    initial, last = (max(0, -steps), min(count, count - steps))
    return lax.ppermute(value, axis, [(source, source + steps) for source in range(initial, last)])


def for_sending(x):

    def short(part):
        return part.astype(jnp.bfloat16) if part.dtype == jnp.float32 else part

    return jax.tree.map(short, x)


def phase_table(rows_count, cols_count, modulus):
    rows_index = jnp.arange(rows_count, dtype=jnp.int32)
    cols_index = jnp.arange(cols_count, dtype=jnp.int32)
    angle = (rows_index[:, None] * cols_index[None, :] % modulus).astype(jnp.float32) * (
        2.0 * math.pi / modulus
    )
    return (jnp.cos(angle), jnp.sin(angle))


def across_outer(values, table):
    return jnp.einsum(
        "qab,ak->qkb", values, table, precision=highest, preferred_element_type=jnp.float32
    )


def along_inner(values, table):
    return jnp.einsum(
        "qkb,bj->qkj", values, table, precision=highest, preferred_element_type=jnp.float32
    )


def fourier_rows(real_part, imag_part, sign):
    rows_count, length = real_part.shape
    outer = length // tile_width
    cos_outer, sin_outer = phase_table(outer, outer, outer)
    cos_twist, sin_twist = phase_table(outer, tile_width, length)
    cos_inner, sin_inner = phase_table(tile_width, tile_width, tile_width)
    first_re = real_part.reshape(rows_count, outer, tile_width)
    first_im = imag_part.reshape(rows_count, outer, tile_width)
    section_re = across_outer(first_re, cos_outer) - sign * across_outer(first_im, sin_outer)
    section_im = across_outer(first_im, cos_outer) + sign * across_outer(first_re, sin_outer)
    twist_re = section_re * cos_twist - sign * section_im * sin_twist
    twist_im = section_im * cos_twist + sign * section_re * sin_twist
    final_re = along_inner(twist_re, cos_inner) - sign * along_inner(twist_im, sin_inner)
    final_im = along_inner(twist_im, cos_inner) + sign * along_inner(twist_re, sin_inner)
    unit_scale = 1.0 / math.sqrt(length)
    final_re = jnp.swapaxes(final_re, 1, 2).reshape(rows_count, length) * unit_scale
    final_im = jnp.swapaxes(final_im, 1, 2).reshape(rows_count, length) * unit_scale
    return (final_re, final_im)


def kernel_blocks(kernel_pair):
    real_k = kernel_pair[0]
    imag_k = kernel_pair[1]
    top_row = jnp.stack([real_k, -imag_k], axis=1)
    bottom_row = jnp.stack([imag_k, real_k], axis=1)
    return jnp.stack([top_row, bottom_row], axis=0)


def angle_table(first, second, modulus):
    angle = ((first[:, None] * second[None, :]) % modulus).astype(jnp.float32) * (
        2.0 * math.pi / modulus
    )
    return (jnp.cos(angle), jnp.sin(angle))


def precise(spec, left, right):
    return jnp.einsum(
        spec, left, right, precision=lax.Precision.HIGH, preferred_element_type=jnp.float32
    )


def split_table(spec, values, table):
    high = table.astype(jnp.bfloat16)
    low = (table - high.astype(jnp.float32)).astype(jnp.bfloat16)
    return jnp.einsum(spec, values, high, preferred_element_type=jnp.float32) + jnp.einsum(
        spec, values, low, preferred_element_type=jnp.float32
    )


def per_device(image, wavelet_dual, weights, kernels, vis_data, tile_list, tile_count):
    panel_rows, chan_count, grid_width = image.shape
    inner = tile_width
    outer = grid_width // inner
    unit_scale = 1.0 / math.sqrt(grid_width)
    bf = jnp.bfloat16
    f32 = jnp.float32
    own_list = tile_list[0, 0]
    own_count = tile_count[0, 0]
    slots_count = own_list.shape[0]
    image_t = jnp.transpose(
        image.astype(bf).reshape(panel_rows, chan_count, inner, outer), (3, 1, 0, 2)
    )
    gathered = lax.all_gather(image_t, "vis", axis=0)
    blocks = gathered.shape[0]
    inner_index = jnp.arange(inner, dtype=jnp.int32)
    outer_index = jnp.arange(outer, dtype=jnp.int32)
    cos_in, sin_in = angle_table(inner_index, inner_index, inner)
    cos_tw, sin_tw = angle_table(outer_index, inner_index, grid_width)
    cos_sel, sin_sel = angle_table(outer_index, own_list, outer)
    stage_re = split_table("vacrb,bk->vacrk", gathered, cos_in)
    stage_im = -split_table("vacrb,bk->vacrk", gathered, sin_in)
    tw_c = cos_tw[None, :, None, None, :]
    tw_s = sin_tw[None, :, None, None, :]
    twist_re = stage_re * tw_c + stage_im * tw_s
    twist_im = stage_im * tw_c - stage_re * tw_s
    sel_c = (cos_sel * unit_scale)
    sel_s = (sin_sel * unit_scale)
    tre = twist_re
    tim = twist_im
    tile_re = precise("as,vacrk->scvrk", sel_c, tre) + precise("as,vacrk->scvrk", sel_s, tim)
    tile_im = precise("as,vacrk->scvrk", sel_c, tim) - precise("as,vacrk->scvrk", sel_s, tre)
    tiles = jnp.stack([tile_re, tile_im], axis=0).astype(bf)
    stacked = kernel_blocks(kernels[0, 0]).reshape(2, -1, 2, blocks, panel_rows)
    predicted = jnp.einsum(
        "omivr,iscvrn->cosmn", stacked, tiles, preferred_element_type=f32
    )
    own_data = vis_data[0, 0]
    live_slots = (jnp.arange(slots_count, dtype=jnp.int32) < own_count)[None, None, :, None, None]
    residual = jnp.where(live_slots, predicted - own_data.astype(f32), 0.0).astype(bf)
    partial = jnp.einsum(
        "omivr,cosmn->iscvrn", stacked, residual, preferred_element_type=f32
    ).astype(bf)
    inv_c = jnp.transpose(cos_sel)
    inv_s = jnp.transpose(sin_sel)
    part_re = partial[0].astype(f32)
    part_im = partial[1].astype(f32)
    back_re = precise("sa,scvrk->vacrk", inv_c, part_re) - precise("sa,scvrk->vacrk", inv_s, part_im)
    back_im = precise("sa,scvrk->vacrk", inv_s, part_re) + precise("sa,scvrk->vacrk", inv_c, part_im)
    turned_re = back_re * tw_c - back_im * tw_s
    turned_im = back_re * tw_s + back_im * tw_c
    out_c = cos_in * unit_scale
    out_s = sin_in * unit_scale
    rows_part = precise("vacrk,kb->vacrb", turned_re, out_c) - precise("vacrk,kb->vacrb", turned_im, out_s)
    rows_sum = lax.psum_scatter(rows_part.astype(bf), "vis", scatter_dimension=0, tiled=True)
    gradient = (
        jnp.transpose(rows_sum[0].astype(f32), (2, 1, 3, 0))
        .reshape(panel_rows, chan_count, grid_width)
    )
    upper_rim = shifted(
        wavelet_dual[panel_rows - 3 :].astype(jnp.bfloat16), ("facet", "vis"), 1
    ).astype(jnp.float32)
    padded_dual = jnp.concatenate([upper_rim, wavelet_dual], axis=0)
    synthesized = jnp.zeros_like(wavelet_dual)
    for offset in range(4):
        synthesized = (
            synthesized + high_taps[offset] * padded_dual[3 - offset : 3 - offset + panel_rows]
        )
    image_next = jnp.maximum(image - primal_step * (gradient + synthesized), 0.0)
    extrap = 2.0 * image_next - image
    lower_rim = shifted(for_sending(extrap[:3]), ("facet", "vis"), -1)
    padded_next = jnp.concatenate([extrap, lower_rim], axis=0)
    detail = jnp.zeros_like(extrap)
    for offset in range(4):
        detail = detail + high_taps[offset] * padded_next[offset : offset + panel_rows]
    update = wavelet_dual + dual_step * detail
    own_energy = jnp.sum(update * update, axis=1)
    other_energy = lax.ppermute(own_energy.astype(bf), "spec", [(0, 1), (1, 0)])
    energy = own_energy + other_energy.astype(f32)
    dual_next = update * weights[:, None, :] / jnp.maximum(weights, jnp.sqrt(energy))[:, None, :]
    return (image_next, dual_next)


def solution(mesh):
    return jax.shard_map(
        per_device,
        mesh=mesh,
        in_specs=(
            P(("facet", "vis"), "spec", None),
            P(("facet", "vis"), "spec", None),
            P(("facet", "vis"), None),
            P("facet", "vis", None, None, None),
            P("facet", "vis", "spec", None, None, None, None),
            P("facet", "vis", None),
            P("facet", "vis"),
        ),
        out_specs=(P(("facet", "vis"), "spec", None), P(("facet", "vis"), "spec", None)),
        check_vma=False,
    )
```

```python
import math

import jax
import jax.numpy as jnp
from jax import lax
from jax.sharding import PartitionSpec as P

root_three = math.sqrt(3.0)
norm_factor = 4.0 * math.sqrt(2.0)
low_taps = [
    (1.0 + root_three) / norm_factor,
    (3.0 + root_three) / norm_factor,
    (3.0 - root_three) / norm_factor,
    (1.0 - root_three) / norm_factor,
]
high_taps = [low_taps[3], -low_taps[2], low_taps[1], -low_taps[0]]
primal_step = 0.2
dual_step = 0.5
tile_width = 128
highest = lax.Precision.HIGHEST


def shifted(value, axis, steps):
    count = lax.axis_size(axis)
    initial, last = (max(0, -steps), min(count, count - steps))
    return lax.ppermute(value, axis, [(source, source + steps) for source in range(initial, last)])


def for_sending(x):

    def short(part):
        return part.astype(jnp.bfloat16) if part.dtype == jnp.float32 else part

    return jax.tree.map(short, x)


def phase_table(rows_count, cols_count, modulus):
    rows_index = jnp.arange(rows_count, dtype=jnp.int32)
    cols_index = jnp.arange(cols_count, dtype=jnp.int32)
    angle = (rows_index[:, None] * cols_index[None, :] % modulus).astype(jnp.float32) * (
        2.0 * math.pi / modulus
    )
    return (jnp.cos(angle), jnp.sin(angle))


def across_outer(values, table):
    return jnp.einsum(
        "qab,ak->qkb", values, table, precision=highest, preferred_element_type=jnp.float32
    )


def along_inner(values, table):
    return jnp.einsum(
        "qkb,bj->qkj", values, table, precision=highest, preferred_element_type=jnp.float32
    )


def fourier_rows(real_part, imag_part, sign):
    rows_count, length = real_part.shape
    outer = length // tile_width
    cos_outer, sin_outer = phase_table(outer, outer, outer)
    cos_twist, sin_twist = phase_table(outer, tile_width, length)
    cos_inner, sin_inner = phase_table(tile_width, tile_width, tile_width)
    first_re = real_part.reshape(rows_count, outer, tile_width)
    first_im = imag_part.reshape(rows_count, outer, tile_width)
    section_re = across_outer(first_re, cos_outer) - sign * across_outer(first_im, sin_outer)
    section_im = across_outer(first_im, cos_outer) + sign * across_outer(first_re, sin_outer)
    twist_re = section_re * cos_twist - sign * section_im * sin_twist
    twist_im = section_im * cos_twist + sign * section_re * sin_twist
    final_re = along_inner(twist_re, cos_inner) - sign * along_inner(twist_im, sin_inner)
    final_im = along_inner(twist_im, cos_inner) + sign * along_inner(twist_re, sin_inner)
    unit_scale = 1.0 / math.sqrt(length)
    final_re = jnp.swapaxes(final_re, 1, 2).reshape(rows_count, length) * unit_scale
    final_im = jnp.swapaxes(final_im, 1, 2).reshape(rows_count, length) * unit_scale
    return (final_re, final_im)


def kernel_blocks(kernel_pair):
    real_k = kernel_pair[0]
    imag_k = kernel_pair[1]
    top_row = jnp.stack([real_k, -imag_k], axis=1)
    bottom_row = jnp.stack([imag_k, real_k], axis=1)
    return jnp.stack([top_row, bottom_row], axis=0)


def angle_table(first, second, modulus):
    angle = ((first[:, None] * second[None, :]) % modulus).astype(jnp.float32) * (
        2.0 * math.pi / modulus
    )
    return (jnp.cos(angle), jnp.sin(angle))


def precise(spec, left, right):
    return jnp.einsum(
        spec, left, right, precision=lax.Precision.HIGH, preferred_element_type=jnp.float32
    )


def split_table(spec, values, table):
    high = table.astype(jnp.bfloat16)
    low = (table - high.astype(jnp.float32)).astype(jnp.bfloat16)
    return jnp.einsum(spec, values, high, preferred_element_type=jnp.float32) + jnp.einsum(
        spec, values, low, preferred_element_type=jnp.float32
    )


def per_device(image, wavelet_dual, weights, kernels, vis_data, tile_list, tile_count):
    panel_rows, chan_count, grid_width = image.shape
    inner = tile_width
    outer = grid_width // inner
    unit_scale = 1.0 / math.sqrt(grid_width)
    bf = jnp.bfloat16
    f32 = jnp.float32
    own_list = tile_list[0, 0]
    own_count = tile_count[0, 0]
    slots_count = own_list.shape[0]
    image_t = jnp.transpose(
        image.astype(bf).reshape(panel_rows, chan_count, inner, outer), (3, 1, 0, 2)
    )
    gathered = lax.all_gather(image_t, "vis", axis=2)
    blocks = gathered.shape[2]
    inner_index = jnp.arange(inner, dtype=jnp.int32)
    outer_index = jnp.arange(outer, dtype=jnp.int32)
    column = outer_index[:, None, None] + outer * inner_index[None, :, None]
    phase = ((column * inner_index[None, None, :]) % grid_width).astype(f32) * (2.0 * math.pi / grid_width)
    dft = jnp.concatenate([jnp.cos(phase), -jnp.sin(phase)], axis=2)
    cos_sel, sin_sel = angle_table(outer_index, own_list, outer)
    spectrum = precise("acvrb,abk->acvrk", gathered.astype(f32), dft)
    part_re = spectrum[..., :inner]
    part_im = spectrum[..., inner:]
    sel_c = cos_sel * unit_scale
    sel_s = sin_sel * unit_scale
    tile_re = precise("as,acvrk->scvrk", sel_c, part_re) + precise("as,acvrk->scvrk", sel_s, part_im)
    tile_im = precise("as,acvrk->scvrk", sel_c, part_im) - precise("as,acvrk->scvrk", sel_s, part_re)
    tiles = jnp.stack([tile_re, tile_im], axis=0).astype(bf)
    stacked = kernel_blocks(kernels[0, 0]).reshape(2, -1, 2, blocks, panel_rows)
    predicted = jnp.einsum(
        "omivr,iscvrn->cosmn", stacked, tiles, preferred_element_type=f32
    )
    own_data = vis_data[0, 0]
    live_slots = (jnp.arange(slots_count, dtype=jnp.int32) < own_count)[None, None, :, None, None]
    residual = jnp.where(live_slots, predicted - own_data.astype(f32), 0.0).astype(bf)
    partial = jnp.einsum(
        "omivr,cosmn->iscvrn", stacked, residual, preferred_element_type=f32
    ).astype(bf)
    inv_c = jnp.transpose(cos_sel)
    inv_s = jnp.transpose(sin_sel)
    grid_re = partial[0].astype(f32)
    grid_im = partial[1].astype(f32)
    back_re = precise("sa,scvrk->acvrk", inv_c, grid_re) - precise("sa,scvrk->acvrk", inv_s, grid_im)
    back_im = precise("sa,scvrk->acvrk", inv_s, grid_re) + precise("sa,scvrk->acvrk", inv_c, grid_im)
    back = jnp.concatenate([back_re, back_im], axis=4)
    idft = jnp.concatenate(
        [jnp.transpose(jnp.cos(phase), (0, 2, 1)), -jnp.transpose(jnp.sin(phase), (0, 2, 1))], axis=1
    ) * unit_scale
    rows_part = precise("acvrk,akb->vacrb", back, idft)
    rows_sum = lax.psum_scatter(rows_part.astype(bf), "vis", scatter_dimension=0, tiled=True)
    gradient = (
        jnp.transpose(rows_sum[0].astype(f32), (2, 1, 3, 0))
        .reshape(panel_rows, chan_count, grid_width)
    )
    upper_rim = shifted(
        wavelet_dual[panel_rows - 3 :].astype(jnp.bfloat16), ("facet", "vis"), 1
    ).astype(jnp.float32)
    padded_dual = jnp.concatenate([upper_rim, wavelet_dual], axis=0)
    synthesized = jnp.zeros_like(wavelet_dual)
    for offset in range(4):
        synthesized = (
            synthesized + high_taps[offset] * padded_dual[3 - offset : 3 - offset + panel_rows]
        )
    image_next = jnp.maximum(image - primal_step * (gradient + synthesized), 0.0)
    extrap = 2.0 * image_next - image
    lower_rim = shifted(for_sending(extrap[:3]), ("facet", "vis"), -1)
    padded_next = jnp.concatenate([extrap, lower_rim], axis=0)
    detail = jnp.zeros_like(extrap)
    for offset in range(4):
        detail = detail + high_taps[offset] * padded_next[offset : offset + panel_rows]
    update = wavelet_dual + dual_step * detail
    own_energy = jnp.sum(update * update, axis=1)
    other_energy = lax.ppermute(own_energy.astype(bf), "spec", [(0, 1), (1, 0)])
    energy = own_energy + other_energy.astype(f32)
    dual_next = update * weights[:, None, :] / jnp.maximum(weights, jnp.sqrt(energy))[:, None, :]
    return (image_next, dual_next)


def solution(mesh):
    return jax.shard_map(
        per_device,
        mesh=mesh,
        in_specs=(
            P(("facet", "vis"), "spec", None),
            P(("facet", "vis"), "spec", None),
            P(("facet", "vis"), None),
            P("facet", "vis", None, None, None),
            P("facet", "vis", "spec", None, None, None, None),
            P("facet", "vis", None),
            P("facet", "vis"),
        ),
        out_specs=(P(("facet", "vis"), "spec", None), P(("facet", "vis"), "spec", None)),
        check_vma=False,
    )
```

```python
import math

import jax
import jax.numpy as jnp
from jax import lax
from jax.sharding import PartitionSpec as P

root_three = math.sqrt(3.0)
norm_factor = 4.0 * math.sqrt(2.0)
low_taps = [
    (1.0 + root_three) / norm_factor,
    (3.0 + root_three) / norm_factor,
    (3.0 - root_three) / norm_factor,
    (1.0 - root_three) / norm_factor,
]
high_taps = [low_taps[3], -low_taps[2], low_taps[1], -low_taps[0]]
primal_step = 0.2
dual_step = 0.5
tile_width = 128
highest = lax.Precision.HIGHEST


def shifted(value, axis, steps):
    count = lax.axis_size(axis)
    initial, last = (max(0, -steps), min(count, count - steps))
    return lax.ppermute(value, axis, [(source, source + steps) for source in range(initial, last)])


def for_sending(x):

    def short(part):
        return part.astype(jnp.bfloat16) if part.dtype == jnp.float32 else part

    return jax.tree.map(short, x)


def phase_table(rows_count, cols_count, modulus):
    rows_index = jnp.arange(rows_count, dtype=jnp.int32)
    cols_index = jnp.arange(cols_count, dtype=jnp.int32)
    angle = (rows_index[:, None] * cols_index[None, :] % modulus).astype(jnp.float32) * (
        2.0 * math.pi / modulus
    )
    return (jnp.cos(angle), jnp.sin(angle))


def across_outer(values, table):
    return jnp.einsum(
        "qab,ak->qkb", values, table, precision=highest, preferred_element_type=jnp.float32
    )


def along_inner(values, table):
    return jnp.einsum(
        "qkb,bj->qkj", values, table, precision=highest, preferred_element_type=jnp.float32
    )


def fourier_rows(real_part, imag_part, sign):
    rows_count, length = real_part.shape
    outer = length // tile_width
    cos_outer, sin_outer = phase_table(outer, outer, outer)
    cos_twist, sin_twist = phase_table(outer, tile_width, length)
    cos_inner, sin_inner = phase_table(tile_width, tile_width, tile_width)
    first_re = real_part.reshape(rows_count, outer, tile_width)
    first_im = imag_part.reshape(rows_count, outer, tile_width)
    section_re = across_outer(first_re, cos_outer) - sign * across_outer(first_im, sin_outer)
    section_im = across_outer(first_im, cos_outer) + sign * across_outer(first_re, sin_outer)
    twist_re = section_re * cos_twist - sign * section_im * sin_twist
    twist_im = section_im * cos_twist + sign * section_re * sin_twist
    final_re = along_inner(twist_re, cos_inner) - sign * along_inner(twist_im, sin_inner)
    final_im = along_inner(twist_im, cos_inner) + sign * along_inner(twist_re, sin_inner)
    unit_scale = 1.0 / math.sqrt(length)
    final_re = jnp.swapaxes(final_re, 1, 2).reshape(rows_count, length) * unit_scale
    final_im = jnp.swapaxes(final_im, 1, 2).reshape(rows_count, length) * unit_scale
    return (final_re, final_im)


def kernel_blocks(kernel_pair):
    real_k = kernel_pair[0]
    imag_k = kernel_pair[1]
    top_row = jnp.stack([real_k, -imag_k], axis=1)
    bottom_row = jnp.stack([imag_k, real_k], axis=1)
    return jnp.stack([top_row, bottom_row], axis=0)


def angle_table(first, second, modulus):
    angle = ((first[:, None] * second[None, :]) % modulus).astype(jnp.float32) * (
        2.0 * math.pi / modulus
    )
    return (jnp.cos(angle), jnp.sin(angle))


def precise(spec, left, right):
    return jnp.einsum(
        spec, left, right, precision=lax.Precision.HIGH, preferred_element_type=jnp.float32
    )


def split_table(spec, values, table):
    high = table.astype(jnp.bfloat16)
    low = (table - high.astype(jnp.float32)).astype(jnp.bfloat16)
    return jnp.einsum(spec, values, high, preferred_element_type=jnp.float32) + jnp.einsum(
        spec, values, low, preferred_element_type=jnp.float32
    )


def per_device(image, wavelet_dual, weights, kernels, vis_data, tile_list, tile_count):
    panel_rows, chan_count, grid_width = image.shape
    inner = tile_width
    outer = grid_width // inner
    unit_scale = 1.0 / math.sqrt(grid_width)
    bf = jnp.bfloat16
    f32 = jnp.float32
    own_list = tile_list[0, 0]
    own_count = tile_count[0, 0]
    slots_count = own_list.shape[0]
    image_rows = image.reshape(panel_rows * chan_count, grid_width)
    grid_re, grid_im = fourier_rows(image_rows, jnp.zeros_like(image_rows), -1.0)
    grid_panel = (
        jnp.stack([grid_re, grid_im], axis=1)
        .reshape(panel_rows, chan_count, 2, grid_width)
        .astype(bf)
    )
    gathered = lax.all_gather(grid_panel, "vis", axis=0, tiled=True)
    facet_rows = gathered.shape[0]
    split_rows = gathered.reshape(facet_rows, chan_count, 2, outer, inner)
    tiles = jnp.take(split_rows, own_list, axis=3)
    stacked = kernel_blocks(kernels[0, 0])
    predicted = jnp.einsum(
        "omir,rcisn->cosmn", stacked, tiles, preferred_element_type=f32
    )
    own_data = vis_data[0, 0]
    live_slots = (jnp.arange(slots_count, dtype=jnp.int32) < own_count)[None, None, :, None, None]
    residual = jnp.where(live_slots, predicted - own_data.astype(f32), 0.0).astype(bf)
    blocks = facet_rows // panel_rows
    stacked5 = stacked.reshape(2, -1, 2, blocks, panel_rows)
    partial = jnp.einsum(
        "omivr,cosmn->iscvrn", stacked5, residual, preferred_element_type=f32
    ).astype(bf)
    inner_index = jnp.arange(inner, dtype=jnp.int32)
    outer_index = jnp.arange(outer, dtype=jnp.int32)
    cos_in, sin_in = angle_table(inner_index, inner_index, inner)
    cos_tw, sin_tw = angle_table(outer_index, inner_index, grid_width)
    cos_sel, sin_sel = angle_table(outer_index, own_list, outer)
    tw_c = cos_tw[None, :, None, None, :]
    tw_s = sin_tw[None, :, None, None, :]
    inv_c = jnp.transpose(cos_sel).astype(bf)
    inv_s = jnp.transpose(sin_sel).astype(bf)
    back_re = jnp.einsum("sa,scvrk->vacrk", inv_c, partial[0], preferred_element_type=f32) - jnp.einsum(
        "sa,scvrk->vacrk", inv_s, partial[1], preferred_element_type=f32
    )
    back_im = jnp.einsum("sa,scvrk->vacrk", inv_s, partial[0], preferred_element_type=f32) + jnp.einsum(
        "sa,scvrk->vacrk", inv_c, partial[1], preferred_element_type=f32
    )
    turned_re = (back_re * tw_c - back_im * tw_s).astype(bf)
    turned_im = (back_re * tw_s + back_im * tw_c).astype(bf)
    out_c = (cos_in * unit_scale).astype(bf)
    out_s = (sin_in * unit_scale).astype(bf)
    rows_part = jnp.einsum("vacrk,kb->vacrb", turned_re, out_c, preferred_element_type=f32) - jnp.einsum(
        "vacrk,kb->vacrb", turned_im, out_s, preferred_element_type=f32
    )
    rows_sum = lax.psum_scatter(rows_part.astype(bf), "vis", scatter_dimension=0, tiled=True)
    gradient = (
        jnp.transpose(rows_sum[0].astype(f32), (2, 1, 3, 0))
        .reshape(panel_rows, chan_count, grid_width)
    )
    upper_rim = shifted(
        wavelet_dual[panel_rows - 3 :].astype(jnp.bfloat16), ("facet", "vis"), 1
    ).astype(jnp.float32)
    padded_dual = jnp.concatenate([upper_rim, wavelet_dual], axis=0)
    synthesized = jnp.zeros_like(wavelet_dual)
    for offset in range(4):
        synthesized = (
            synthesized + high_taps[offset] * padded_dual[3 - offset : 3 - offset + panel_rows]
        )
    image_next = jnp.maximum(image - primal_step * (gradient + synthesized), 0.0)
    extrap = 2.0 * image_next - image
    lower_rim = shifted(for_sending(extrap[:3]), ("facet", "vis"), -1)
    padded_next = jnp.concatenate([extrap, lower_rim], axis=0)
    detail = jnp.zeros_like(extrap)
    for offset in range(4):
        detail = detail + high_taps[offset] * padded_next[offset : offset + panel_rows]
    update = wavelet_dual + dual_step * detail
    own_energy = jnp.sum(update * update, axis=1)
    other_energy = lax.ppermute(own_energy.astype(bf), "spec", [(0, 1), (1, 0)])
    energy = own_energy + other_energy.astype(f32)
    dual_next = update * weights[:, None, :] / jnp.maximum(weights, jnp.sqrt(energy))[:, None, :]
    return (image_next, dual_next)


def solution(mesh):
    return jax.shard_map(
        per_device,
        mesh=mesh,
        in_specs=(
            P(("facet", "vis"), "spec", None),
            P(("facet", "vis"), "spec", None),
            P(("facet", "vis"), None),
            P("facet", "vis", None, None, None),
            P("facet", "vis", "spec", None, None, None, None),
            P("facet", "vis", None),
            P("facet", "vis"),
        ),
        out_specs=(P(("facet", "vis"), "spec", None), P(("facet", "vis"), "spec", None)),
        check_vma=False,
    )
```

```python
import math

import jax
import jax.numpy as jnp
from jax import lax
from jax.sharding import PartitionSpec as P
from jax.experimental import pallas as pl
from jax.experimental.pallas import tpu as pltpu

root_three = math.sqrt(3.0)
norm_factor = 4.0 * math.sqrt(2.0)
low_taps = [
    (1.0 + root_three) / norm_factor,
    (3.0 + root_three) / norm_factor,
    (3.0 - root_three) / norm_factor,
    (1.0 - root_three) / norm_factor,
]
high_taps = [low_taps[3], -low_taps[2], low_taps[1], -low_taps[0]]
primal_step = 0.2
dual_step = 0.5
tile_width = 128
highest = lax.Precision.HIGHEST


def shifted(value, axis, steps):
    count = lax.axis_size(axis)
    initial, last = (max(0, -steps), min(count, count - steps))
    return lax.ppermute(value, axis, [(source, source + steps) for source in range(initial, last)])


def for_sending(x):

    def short(part):
        return part.astype(jnp.bfloat16) if part.dtype == jnp.float32 else part

    return jax.tree.map(short, x)


def phase_table(rows_count, cols_count, modulus):
    rows_index = jnp.arange(rows_count, dtype=jnp.int32)
    cols_index = jnp.arange(cols_count, dtype=jnp.int32)
    angle = (rows_index[:, None] * cols_index[None, :] % modulus).astype(jnp.float32) * (
        2.0 * math.pi / modulus
    )
    return (jnp.cos(angle), jnp.sin(angle))


def across_outer(values, table):
    return jnp.einsum(
        "qab,ak->qkb", values, table, precision=highest, preferred_element_type=jnp.float32
    )


def along_inner(values, table):
    return jnp.einsum(
        "qkb,bj->qkj", values, table, precision=highest, preferred_element_type=jnp.float32
    )


def fourier_rows(real_part, imag_part, sign):
    rows_count, length = real_part.shape
    outer = length // tile_width
    cos_outer, sin_outer = phase_table(outer, outer, outer)
    cos_twist, sin_twist = phase_table(outer, tile_width, length)
    cos_inner, sin_inner = phase_table(tile_width, tile_width, tile_width)
    first_re = real_part.reshape(rows_count, outer, tile_width)
    first_im = imag_part.reshape(rows_count, outer, tile_width)
    section_re = across_outer(first_re, cos_outer) - sign * across_outer(first_im, sin_outer)
    section_im = across_outer(first_im, cos_outer) + sign * across_outer(first_re, sin_outer)
    twist_re = section_re * cos_twist - sign * section_im * sin_twist
    twist_im = section_im * cos_twist + sign * section_re * sin_twist
    final_re = along_inner(twist_re, cos_inner) - sign * along_inner(twist_im, sin_inner)
    final_im = along_inner(twist_im, cos_inner) + sign * along_inner(twist_re, sin_inner)
    unit_scale = 1.0 / math.sqrt(length)
    final_re = jnp.swapaxes(final_re, 1, 2).reshape(rows_count, length) * unit_scale
    final_im = jnp.swapaxes(final_im, 1, 2).reshape(rows_count, length) * unit_scale
    return (final_re, final_im)


def kernel_blocks(kernel_pair):
    real_k = kernel_pair[0]
    imag_k = kernel_pair[1]
    top_row = jnp.stack([real_k, -imag_k], axis=1)
    bottom_row = jnp.stack([imag_k, real_k], axis=1)
    return jnp.stack([top_row, bottom_row], axis=0)


def angle_table(first, second, modulus):
    angle = ((first[:, None] * second[None, :]) % modulus).astype(jnp.float32) * (
        2.0 * math.pi / modulus
    )
    return (jnp.cos(angle), jnp.sin(angle))


def precise(spec, left, right):
    return jnp.einsum(
        spec, left, right, precision=lax.Precision.HIGH, preferred_element_type=jnp.float32
    )


def split_table(spec, values, table):
    high = table.astype(jnp.bfloat16)
    low = (table - high.astype(jnp.float32)).astype(jnp.bfloat16)
    return jnp.einsum(spec, values, high, preferred_element_type=jnp.float32) + jnp.einsum(
        spec, values, low, preferred_element_type=jnp.float32
    )


def degrid_body(list_ref, count_ref, kmat_ref, kadj_ref, grid_ref, vis_ref, out_ref):
    slot = pl.program_id(1)

    @pl.when(slot < count_ref[0])
    def _():
        rows = grid_ref.shape[0] * grid_ref.shape[1] * grid_ref.shape[2]
        tile = grid_ref[...].astype(jnp.float32).reshape(rows, grid_ref.shape[3]).astype(jnp.bfloat16)
        predicted = jnp.dot(kmat_ref[...], tile, preferred_element_type=jnp.float32)
        measured = vis_ref[...].astype(jnp.float32).reshape(predicted.shape)
        residual = (predicted - measured).astype(jnp.bfloat16)
        gridded = jnp.dot(kadj_ref[...], residual, preferred_element_type=jnp.float32)
        out_ref[...] = gridded.astype(out_ref.dtype)

    @pl.when(slot >= count_ref[0])
    def _():
        out_ref[...] = jnp.zeros_like(out_ref)


def degrid_grid(own_list, own_count, kernel_mat, kernel_adj, gathered, own_data):
    blocks, chans, parts, rows, width = gathered.shape
    slots = own_list.shape[0]
    out_rows, in_rows = kernel_mat.shape
    inner = tile_width
    flops = 4 * out_rows * in_rows * inner * chans * slots
    return pl.pallas_call(
        degrid_body,
        grid_spec=pltpu.PrefetchScalarGridSpec(
            num_scalar_prefetch=2,
            grid=(chans, slots),
            in_specs=[
                pl.BlockSpec((out_rows, in_rows), lambda c, s, lst, cnt: (0, 0)),
                pl.BlockSpec((in_rows, out_rows), lambda c, s, lst, cnt: (0, 0)),
                pl.BlockSpec(
                    (blocks, None, parts, rows, inner), lambda c, s, lst, cnt: (0, c, 0, 0, lst[s])
                ),
                pl.BlockSpec(
                    (None, parts, None, out_rows // parts, inner),
                    lambda c, s, lst, cnt: (c, 0, s, 0, 0),
                ),
            ],
            out_specs=pl.BlockSpec((None, None, in_rows, inner), lambda c, s, lst, cnt: (c, s, 0, 0)),
        ),
        out_shape=jax.ShapeDtypeStruct((chans, slots, in_rows, inner), jnp.bfloat16),
        cost_estimate=pl.CostEstimate(
            flops=flops, bytes_accessed=2 * chans * slots * (out_rows + 2 * in_rows) * inner,
            transcendentals=0,
        ),
    )(own_list, own_count, kernel_mat, kernel_adj, gathered, own_data)


def per_device(image, wavelet_dual, weights, kernels, vis_data, tile_list, tile_count):
    panel_rows, chan_count, grid_width = image.shape
    inner = tile_width
    outer = grid_width // inner
    unit_scale = 1.0 / math.sqrt(grid_width)
    bf = jnp.bfloat16
    f32 = jnp.float32
    own_list = tile_list[0, 0]
    own_count = tile_count[0, 0]
    slots_count = own_list.shape[0]
    image_rows = image.reshape(panel_rows * chan_count, grid_width)
    grid_re, grid_im = fourier_rows(image_rows, jnp.zeros_like(image_rows), -1.0)
    grid_panel = (
        jnp.stack([grid_re, grid_im], axis=1)
        .reshape(panel_rows, chan_count, 2, grid_width)
        .astype(bf)
    )
    panel_t = jnp.transpose(grid_panel, (1, 2, 0, 3))
    gathered = lax.all_gather(panel_t, "vis", axis=0)
    blocks = gathered.shape[0]
    stacked = kernel_blocks(kernels[0, 0])
    out_rows, vis_rows = stacked.shape[0] * stacked.shape[1], stacked.shape[2] * blocks * panel_rows
    kernel_mat = jnp.transpose(
        stacked.reshape(2, -1, 2, blocks, panel_rows), (0, 1, 3, 2, 4)
    ).reshape(out_rows, vis_rows)
    kernel_adj = jnp.transpose(kernel_mat)
    own_data = vis_data[0, 0]
    partial = degrid_grid(own_list, own_count.reshape(1), kernel_mat, kernel_adj, gathered, own_data)
    partial = partial.reshape(chan_count, slots_count, blocks, 2, panel_rows, inner)
    inner_index = jnp.arange(inner, dtype=jnp.int32)
    outer_index = jnp.arange(outer, dtype=jnp.int32)
    cos_in, sin_in = angle_table(inner_index, inner_index, inner)
    cos_tw, sin_tw = angle_table(outer_index, inner_index, grid_width)
    cos_sel, sin_sel = angle_table(outer_index, own_list, outer)
    tw_c = cos_tw[None, :, None, None, :]
    tw_s = sin_tw[None, :, None, None, :]
    inv_c = jnp.transpose(cos_sel).astype(bf)
    inv_s = jnp.transpose(sin_sel).astype(bf)
    part_re = partial[:, :, :, 0]
    part_im = partial[:, :, :, 1]
    back_re = jnp.einsum("sa,csvrk->vacrk", inv_c, part_re, preferred_element_type=f32) - jnp.einsum(
        "sa,csvrk->vacrk", inv_s, part_im, preferred_element_type=f32
    )
    back_im = jnp.einsum("sa,csvrk->vacrk", inv_s, part_re, preferred_element_type=f32) + jnp.einsum(
        "sa,csvrk->vacrk", inv_c, part_im, preferred_element_type=f32
    )
    turned_re = (back_re * tw_c - back_im * tw_s).astype(bf)
    turned_im = (back_re * tw_s + back_im * tw_c).astype(bf)
    out_c = (cos_in * unit_scale).astype(bf)
    out_s = (sin_in * unit_scale).astype(bf)
    rows_part = jnp.einsum("vacrk,kb->vacrb", turned_re, out_c, preferred_element_type=f32) - jnp.einsum(
        "vacrk,kb->vacrb", turned_im, out_s, preferred_element_type=f32
    )
    rows_sum = lax.psum_scatter(rows_part.astype(bf), "vis", scatter_dimension=0, tiled=True)
    gradient = (
        jnp.transpose(rows_sum[0].astype(f32), (2, 1, 3, 0))
        .reshape(panel_rows, chan_count, grid_width)
    )
    upper_rim = shifted(
        wavelet_dual[panel_rows - 3 :].astype(jnp.bfloat16), ("facet", "vis"), 1
    ).astype(jnp.float32)
    padded_dual = jnp.concatenate([upper_rim, wavelet_dual], axis=0)
    synthesized = jnp.zeros_like(wavelet_dual)
    for offset in range(4):
        synthesized = (
            synthesized + high_taps[offset] * padded_dual[3 - offset : 3 - offset + panel_rows]
        )
    image_next = jnp.maximum(image - primal_step * (gradient + synthesized), 0.0)
    extrap = 2.0 * image_next - image
    lower_rim = shifted(for_sending(extrap[:3]), ("facet", "vis"), -1)
    padded_next = jnp.concatenate([extrap, lower_rim], axis=0)
    detail = jnp.zeros_like(extrap)
    for offset in range(4):
        detail = detail + high_taps[offset] * padded_next[offset : offset + panel_rows]
    update = wavelet_dual + dual_step * detail
    own_energy = jnp.sum(update * update, axis=1)
    other_energy = lax.ppermute(own_energy.astype(bf), "spec", [(0, 1), (1, 0)])
    energy = own_energy + other_energy.astype(f32)
    dual_next = update * weights[:, None, :] / jnp.maximum(weights, jnp.sqrt(energy))[:, None, :]
    return (image_next, dual_next)


def solution(mesh):
    return jax.shard_map(
        per_device,
        mesh=mesh,
        in_specs=(
            P(("facet", "vis"), "spec", None),
            P(("facet", "vis"), "spec", None),
            P(("facet", "vis"), None),
            P("facet", "vis", None, None, None),
            P("facet", "vis", "spec", None, None, None, None),
            P("facet", "vis", None),
            P("facet", "vis"),
        ),
        out_specs=(P(("facet", "vis"), "spec", None), P(("facet", "vis"), "spec", None)),
        check_vma=False,
    )
```

```python
import math

import jax
import jax.numpy as jnp
from jax import lax
from jax.sharding import PartitionSpec as P
from jax.experimental import pallas as pl
from jax.experimental.pallas import tpu as pltpu

root_three = math.sqrt(3.0)
norm_factor = 4.0 * math.sqrt(2.0)
low_taps = [
    (1.0 + root_three) / norm_factor,
    (3.0 + root_three) / norm_factor,
    (3.0 - root_three) / norm_factor,
    (1.0 - root_three) / norm_factor,
]
high_taps = [low_taps[3], -low_taps[2], low_taps[1], -low_taps[0]]
primal_step = 0.2
dual_step = 0.5
tile_width = 128
highest = lax.Precision.HIGHEST


def shifted(value, axis, steps):
    count = lax.axis_size(axis)
    initial, last = (max(0, -steps), min(count, count - steps))
    return lax.ppermute(value, axis, [(source, source + steps) for source in range(initial, last)])


def for_sending(x):

    def short(part):
        return part.astype(jnp.bfloat16) if part.dtype == jnp.float32 else part

    return jax.tree.map(short, x)


def phase_table(rows_count, cols_count, modulus):
    rows_index = jnp.arange(rows_count, dtype=jnp.int32)
    cols_index = jnp.arange(cols_count, dtype=jnp.int32)
    angle = (rows_index[:, None] * cols_index[None, :] % modulus).astype(jnp.float32) * (
        2.0 * math.pi / modulus
    )
    return (jnp.cos(angle), jnp.sin(angle))


def across_outer(values, table):
    return jnp.einsum(
        "qab,ak->qkb", values, table, precision=highest, preferred_element_type=jnp.float32
    )


def along_inner(values, table):
    return jnp.einsum(
        "qkb,bj->qkj", values, table, precision=highest, preferred_element_type=jnp.float32
    )


def fourier_rows(real_part, imag_part, sign):
    rows_count, length = real_part.shape
    outer = length // tile_width
    cos_outer, sin_outer = phase_table(outer, outer, outer)
    cos_twist, sin_twist = phase_table(outer, tile_width, length)
    cos_inner, sin_inner = phase_table(tile_width, tile_width, tile_width)
    first_re = real_part.reshape(rows_count, outer, tile_width)
    first_im = imag_part.reshape(rows_count, outer, tile_width)
    section_re = across_outer(first_re, cos_outer) - sign * across_outer(first_im, sin_outer)
    section_im = across_outer(first_im, cos_outer) + sign * across_outer(first_re, sin_outer)
    twist_re = section_re * cos_twist - sign * section_im * sin_twist
    twist_im = section_im * cos_twist + sign * section_re * sin_twist
    final_re = along_inner(twist_re, cos_inner) - sign * along_inner(twist_im, sin_inner)
    final_im = along_inner(twist_im, cos_inner) + sign * along_inner(twist_re, sin_inner)
    unit_scale = 1.0 / math.sqrt(length)
    final_re = jnp.swapaxes(final_re, 1, 2).reshape(rows_count, length) * unit_scale
    final_im = jnp.swapaxes(final_im, 1, 2).reshape(rows_count, length) * unit_scale
    return (final_re, final_im)


def kernel_blocks(kernel_pair):
    real_k = kernel_pair[0]
    imag_k = kernel_pair[1]
    top_row = jnp.stack([real_k, -imag_k], axis=1)
    bottom_row = jnp.stack([imag_k, real_k], axis=1)
    return jnp.stack([top_row, bottom_row], axis=0)


def angle_table(first, second, modulus):
    angle = ((first[:, None] * second[None, :]) % modulus).astype(jnp.float32) * (
        2.0 * math.pi / modulus
    )
    return (jnp.cos(angle), jnp.sin(angle))


def precise(spec, left, right):
    return jnp.einsum(
        spec, left, right, precision=lax.Precision.HIGH, preferred_element_type=jnp.float32
    )


def split_table(spec, values, table):
    high = table.astype(jnp.bfloat16)
    low = (table - high.astype(jnp.float32)).astype(jnp.bfloat16)
    return jnp.einsum(spec, values, high, preferred_element_type=jnp.float32) + jnp.einsum(
        spec, values, low, preferred_element_type=jnp.float32
    )


def degrid_body(list_ref, count_ref, kmat_ref, kadj_ref, grid_ref, vis_ref, out_ref):
    slot = pl.program_id(1)

    @pl.when(slot < count_ref[0])
    def _():
        rows = grid_ref.shape[0] * grid_ref.shape[1] * grid_ref.shape[2]
        tile = grid_ref[...].astype(jnp.float32).reshape(rows, grid_ref.shape[3]).astype(jnp.bfloat16)
        predicted = jnp.dot(kmat_ref[...], tile, preferred_element_type=jnp.float32)
        measured = vis_ref[...].astype(jnp.float32).reshape(predicted.shape)
        residual = (predicted - measured).astype(jnp.bfloat16)
        gridded = jnp.dot(kadj_ref[...], residual, preferred_element_type=jnp.float32)
        out_ref[...] = gridded.astype(out_ref.dtype)

    @pl.when(slot >= count_ref[0])
    def _():
        out_ref[...] = jnp.zeros_like(out_ref)


def degrid_grid(own_list, own_count, kernel_mat, kernel_adj, gathered, own_data):
    blocks, chans, parts, rows, width = gathered.shape
    slots = own_list.shape[0]
    out_rows, in_rows = kernel_mat.shape
    inner = tile_width
    flops = 4 * out_rows * in_rows * inner * chans * slots
    return pl.pallas_call(
        degrid_body,
        grid_spec=pltpu.PrefetchScalarGridSpec(
            num_scalar_prefetch=2,
            grid=(chans, slots),
            in_specs=[
                pl.BlockSpec((out_rows, in_rows), lambda c, s, lst, cnt: (0, 0)),
                pl.BlockSpec((in_rows, out_rows), lambda c, s, lst, cnt: (0, 0)),
                pl.BlockSpec(
                    (blocks, None, parts, rows, inner), lambda c, s, lst, cnt: (0, c, 0, 0, lst[s])
                ),
                pl.BlockSpec(
                    (None, parts, None, out_rows // parts, inner),
                    lambda c, s, lst, cnt: (c, 0, s, 0, 0),
                ),
            ],
            out_specs=pl.BlockSpec((None, None, in_rows, inner), lambda c, s, lst, cnt: (c, s, 0, 0)),
        ),
        out_shape=jax.ShapeDtypeStruct((chans, slots, in_rows, inner), jnp.bfloat16),
        cost_estimate=pl.CostEstimate(
            flops=flops, bytes_accessed=2 * chans * slots * (out_rows + 2 * in_rows) * inner,
            transcendentals=0,
        ),
    )(own_list, own_count, kernel_mat, kernel_adj, gathered, own_data)


def chunk_grid(image):
    panel_rows, chan_count, grid_width = image.shape
    inner = tile_width
    outer = grid_width // inner
    unit_scale = 1.0 / math.sqrt(grid_width)
    bf = jnp.bfloat16
    f32 = jnp.float32
    image_rows = image.reshape(panel_rows * chan_count, grid_width)
    grid_re, grid_im = fourier_rows(image_rows, jnp.zeros_like(image_rows), -1.0)
    grid_panel = (
        jnp.stack([grid_re, grid_im], axis=1)
        .reshape(panel_rows, chan_count, 2, grid_width)
        .astype(bf)
    )
    panel_t = jnp.transpose(grid_panel, (1, 2, 0, 3))
    return lax.all_gather(panel_t, "vis", axis=0)


def chunk_rows(gathered, kernels, own_data, tile_list, tile_count):
    blocks, chan_count, parts, panel_rows, grid_width = gathered.shape
    inner = tile_width
    outer = grid_width // inner
    unit_scale = 1.0 / math.sqrt(grid_width)
    bf = jnp.bfloat16
    f32 = jnp.float32
    own_list = tile_list[0, 0]
    own_count = tile_count[0, 0]
    slots_count = own_list.shape[0]
    blocks = gathered.shape[0]
    stacked = kernel_blocks(kernels[0, 0])
    out_rows, vis_rows = stacked.shape[0] * stacked.shape[1], stacked.shape[2] * blocks * panel_rows
    kernel_mat = jnp.transpose(
        stacked.reshape(2, -1, 2, blocks, panel_rows), (0, 1, 3, 2, 4)
    ).reshape(out_rows, vis_rows)
    kernel_adj = jnp.transpose(kernel_mat)
    partial = degrid_grid(own_list, own_count.reshape(1), kernel_mat, kernel_adj, gathered, own_data)
    partial = partial.reshape(chan_count, slots_count, blocks, 2, panel_rows, inner)
    inner_index = jnp.arange(inner, dtype=jnp.int32)
    outer_index = jnp.arange(outer, dtype=jnp.int32)
    cos_in, sin_in = angle_table(inner_index, inner_index, inner)
    cos_tw, sin_tw = angle_table(outer_index, inner_index, grid_width)
    cos_sel, sin_sel = angle_table(outer_index, own_list, outer)
    tw_c = cos_tw[None, :, None, None, :]
    tw_s = sin_tw[None, :, None, None, :]
    inv_c = jnp.transpose(cos_sel).astype(bf)
    inv_s = jnp.transpose(sin_sel).astype(bf)
    part_re = partial[:, :, :, 0]
    part_im = partial[:, :, :, 1]
    back_re = jnp.einsum("sa,csvrk->vacrk", inv_c, part_re, preferred_element_type=f32) - jnp.einsum(
        "sa,csvrk->vacrk", inv_s, part_im, preferred_element_type=f32
    )
    back_im = jnp.einsum("sa,csvrk->vacrk", inv_s, part_re, preferred_element_type=f32) + jnp.einsum(
        "sa,csvrk->vacrk", inv_c, part_im, preferred_element_type=f32
    )
    turned_re = (back_re * tw_c - back_im * tw_s).astype(bf)
    turned_im = (back_re * tw_s + back_im * tw_c).astype(bf)
    out_c = (cos_in * unit_scale).astype(bf)
    out_s = (sin_in * unit_scale).astype(bf)
    rows_part = jnp.einsum("vacrk,kb->vacrb", turned_re, out_c, preferred_element_type=f32) - jnp.einsum(
        "vacrk,kb->vacrb", turned_im, out_s, preferred_element_type=f32
    )
    return rows_part.astype(bf)


def rows_gradient(rows_part):
    rows_sum = lax.psum_scatter(rows_part, "vis", scatter_dimension=0, tiled=True)
    outer, chan_count, panel_rows, inner = rows_sum.shape[1:]
    return (
        jnp.transpose(rows_sum[0].astype(jnp.float32), (2, 1, 3, 0))
        .reshape(panel_rows, chan_count, outer * inner)
    )


def per_device(image, wavelet_dual, weights, kernels, vis_data, tile_list, tile_count):
    panel_rows, chan_count, grid_width = image.shape
    bf = jnp.bfloat16
    f32 = jnp.float32
    chunks = 2
    width = chan_count // chunks
    grids = [chunk_grid(image[:, part * width : (part + 1) * width]) for part in range(chunks)]
    pieces = []
    for part in range(chunks):
        rows_part = chunk_rows(
            grids[part], kernels, vis_data[0, 0, part * width : (part + 1) * width], tile_list, tile_count
        )
        if part + 1 < chunks:
            rows_part, grids[part + 1] = lax.optimization_barrier((rows_part, grids[part + 1]))
        pieces.append(rows_gradient(rows_part))
    gradient = jnp.concatenate(pieces, axis=1)
    upper_rim = shifted(
        wavelet_dual[panel_rows - 3 :].astype(jnp.bfloat16), ("facet", "vis"), 1
    ).astype(jnp.float32)
    padded_dual = jnp.concatenate([upper_rim, wavelet_dual], axis=0)
    synthesized = jnp.zeros_like(wavelet_dual)
    for offset in range(4):
        synthesized = (
            synthesized + high_taps[offset] * padded_dual[3 - offset : 3 - offset + panel_rows]
        )
    image_next = jnp.maximum(image - primal_step * (gradient + synthesized), 0.0)
    extrap = 2.0 * image_next - image
    lower_rim = shifted(for_sending(extrap[:3]), ("facet", "vis"), -1)
    padded_next = jnp.concatenate([extrap, lower_rim], axis=0)
    detail = jnp.zeros_like(extrap)
    for offset in range(4):
        detail = detail + high_taps[offset] * padded_next[offset : offset + panel_rows]
    update = wavelet_dual + dual_step * detail
    own_energy = jnp.sum(update * update, axis=1)
    other_energy = lax.ppermute(own_energy.astype(bf), "spec", [(0, 1), (1, 0)])
    energy = own_energy + other_energy.astype(f32)
    dual_next = update * weights[:, None, :] / jnp.maximum(weights, jnp.sqrt(energy))[:, None, :]
    return (image_next, dual_next)


def solution(mesh):
    return jax.shard_map(
        per_device,
        mesh=mesh,
        in_specs=(
            P(("facet", "vis"), "spec", None),
            P(("facet", "vis"), "spec", None),
            P(("facet", "vis"), None),
            P("facet", "vis", None, None, None),
            P("facet", "vis", "spec", None, None, None, None),
            P("facet", "vis", None),
            P("facet", "vis"),
        ),
        out_specs=(P(("facet", "vis"), "spec", None), P(("facet", "vis"), "spec", None)),
        check_vma=False,
    )
```

```python
import math

import jax
import jax.numpy as jnp
from jax import lax
from jax.sharding import PartitionSpec as P
from jax.experimental import pallas as pl
from jax.experimental.pallas import tpu as pltpu

root_three = math.sqrt(3.0)
norm_factor = 4.0 * math.sqrt(2.0)
low_taps = [
    (1.0 + root_three) / norm_factor,
    (3.0 + root_three) / norm_factor,
    (3.0 - root_three) / norm_factor,
    (1.0 - root_three) / norm_factor,
]
high_taps = [low_taps[3], -low_taps[2], low_taps[1], -low_taps[0]]
primal_step = 0.2
dual_step = 0.5
tile_width = 128
highest = lax.Precision.HIGHEST


def shifted(value, axis, steps):
    count = lax.axis_size(axis)
    initial, last = (max(0, -steps), min(count, count - steps))
    return lax.ppermute(value, axis, [(source, source + steps) for source in range(initial, last)])


def for_sending(x):

    def short(part):
        return part.astype(jnp.bfloat16) if part.dtype == jnp.float32 else part

    return jax.tree.map(short, x)


def phase_table(rows_count, cols_count, modulus):
    rows_index = jnp.arange(rows_count, dtype=jnp.int32)
    cols_index = jnp.arange(cols_count, dtype=jnp.int32)
    angle = (rows_index[:, None] * cols_index[None, :] % modulus).astype(jnp.float32) * (
        2.0 * math.pi / modulus
    )
    return (jnp.cos(angle), jnp.sin(angle))


def across_outer(values, table):
    return jnp.einsum(
        "qab,ak->qkb", values, table, precision=highest, preferred_element_type=jnp.float32
    )


def along_inner(values, table):
    return jnp.einsum(
        "qkb,bj->qkj", values, table, precision=highest, preferred_element_type=jnp.float32
    )


def fourier_rows(real_part, imag_part, sign):
    rows_count, length = real_part.shape
    outer = length // tile_width
    cos_outer, sin_outer = phase_table(outer, outer, outer)
    cos_twist, sin_twist = phase_table(outer, tile_width, length)
    cos_inner, sin_inner = phase_table(tile_width, tile_width, tile_width)
    first_re = real_part.reshape(rows_count, outer, tile_width)
    first_im = imag_part.reshape(rows_count, outer, tile_width)
    section_re = across_outer(first_re, cos_outer) - sign * across_outer(first_im, sin_outer)
    section_im = across_outer(first_im, cos_outer) + sign * across_outer(first_re, sin_outer)
    twist_re = section_re * cos_twist - sign * section_im * sin_twist
    twist_im = section_im * cos_twist + sign * section_re * sin_twist
    final_re = along_inner(twist_re, cos_inner) - sign * along_inner(twist_im, sin_inner)
    final_im = along_inner(twist_im, cos_inner) + sign * along_inner(twist_re, sin_inner)
    unit_scale = 1.0 / math.sqrt(length)
    final_re = jnp.swapaxes(final_re, 1, 2).reshape(rows_count, length) * unit_scale
    final_im = jnp.swapaxes(final_im, 1, 2).reshape(rows_count, length) * unit_scale
    return (final_re, final_im)


def kernel_blocks(kernel_pair):
    real_k = kernel_pair[0]
    imag_k = kernel_pair[1]
    top_row = jnp.stack([real_k, -imag_k], axis=1)
    bottom_row = jnp.stack([imag_k, real_k], axis=1)
    return jnp.stack([top_row, bottom_row], axis=0)


def angle_table(first, second, modulus):
    angle = ((first[:, None] * second[None, :]) % modulus).astype(jnp.float32) * (
        2.0 * math.pi / modulus
    )
    return (jnp.cos(angle), jnp.sin(angle))


def precise(spec, left, right):
    return jnp.einsum(
        spec, left, right, precision=lax.Precision.HIGH, preferred_element_type=jnp.float32
    )


def split_table(spec, values, table):
    high = table.astype(jnp.bfloat16)
    low = (table - high.astype(jnp.float32)).astype(jnp.bfloat16)
    return jnp.einsum(spec, values, high, preferred_element_type=jnp.float32) + jnp.einsum(
        spec, values, low, preferred_element_type=jnp.float32
    )


def degrid_body(list_ref, count_ref, kmat_ref, kadj_ref, *refs):
    tile_refs, vis_ref, out_ref = refs[:-2], refs[-2], refs[-1]
    group = len(tile_refs)
    step = pl.program_id(1)
    for place, grid_ref in enumerate(tile_refs):
        slot = step * group + place

        @pl.when(slot < count_ref[0])
        def _():
            rows = grid_ref.shape[0] * grid_ref.shape[1] * grid_ref.shape[2]
            tile = grid_ref[...].astype(jnp.float32).reshape(rows, grid_ref.shape[3]).astype(jnp.bfloat16)
            predicted = jnp.dot(kmat_ref[...], tile, preferred_element_type=jnp.float32)
            measured = vis_ref[:, place].astype(jnp.float32).reshape(predicted.shape)
            residual = (predicted - measured).astype(jnp.bfloat16)
            gridded = jnp.dot(kadj_ref[...], residual, preferred_element_type=jnp.float32)
            out_ref[place] = gridded.astype(out_ref.dtype)

        @pl.when(slot >= count_ref[0])
        def _():
            out_ref[place] = jnp.zeros(out_ref.shape[1:], out_ref.dtype)


def tile_spec(blocks, parts, rows, inner, group, place):
    return pl.BlockSpec(
        (blocks, None, parts, rows, inner),
        lambda c, s, lst, cnt: (0, c, 0, 0, lst[s * group + place]),
    )


def degrid_grid(own_list, own_count, kernel_mat, kernel_adj, gathered, own_data):
    blocks, chans, parts, rows, width = gathered.shape
    slots = own_list.shape[0]
    group = 4
    out_rows, in_rows = kernel_mat.shape
    inner = tile_width
    flops = 4 * out_rows * in_rows * inner * chans * slots
    return pl.pallas_call(
        degrid_body,
        grid_spec=pltpu.PrefetchScalarGridSpec(
            num_scalar_prefetch=2,
            grid=(chans, slots // group),
            in_specs=[
                pl.BlockSpec((out_rows, in_rows), lambda c, s, lst, cnt: (0, 0)),
                pl.BlockSpec((in_rows, out_rows), lambda c, s, lst, cnt: (0, 0)),
            ]
            + [tile_spec(blocks, parts, rows, inner, group, place) for place in range(group)]
            + [
                pl.BlockSpec(
                    (None, parts, group, out_rows // parts, inner),
                    lambda c, s, lst, cnt: (c, 0, s, 0, 0),
                ),
            ],
            out_specs=pl.BlockSpec((None, group, in_rows, inner), lambda c, s, lst, cnt: (c, s, 0, 0)),
        ),
        out_shape=jax.ShapeDtypeStruct((chans, slots, in_rows, inner), jnp.bfloat16),
        cost_estimate=pl.CostEstimate(
            flops=flops, bytes_accessed=2 * chans * slots * (out_rows + 2 * in_rows) * inner,
            transcendentals=0,
        ),
    )(own_list, own_count, kernel_mat, kernel_adj, *([gathered] * group), own_data)


def per_device(image, wavelet_dual, weights, kernels, vis_data, tile_list, tile_count):
    panel_rows, chan_count, grid_width = image.shape
    inner = tile_width
    outer = grid_width // inner
    unit_scale = 1.0 / math.sqrt(grid_width)
    bf = jnp.bfloat16
    f32 = jnp.float32
    own_list = tile_list[0, 0]
    own_count = tile_count[0, 0]
    slots_count = own_list.shape[0]
    image_rows = image.reshape(panel_rows * chan_count, grid_width)
    grid_re, grid_im = fourier_rows(image_rows, jnp.zeros_like(image_rows), -1.0)
    grid_panel = (
        jnp.stack([grid_re, grid_im], axis=1)
        .reshape(panel_rows, chan_count, 2, grid_width)
        .astype(bf)
    )
    panel_t = jnp.transpose(grid_panel, (1, 2, 0, 3))
    gathered = lax.all_gather(panel_t, "vis", axis=0)
    blocks = gathered.shape[0]
    stacked = kernel_blocks(kernels[0, 0])
    out_rows, vis_rows = stacked.shape[0] * stacked.shape[1], stacked.shape[2] * blocks * panel_rows
    kernel_mat = jnp.transpose(
        stacked.reshape(2, -1, 2, blocks, panel_rows), (0, 1, 3, 2, 4)
    ).reshape(out_rows, vis_rows)
    kernel_adj = jnp.transpose(kernel_mat)
    own_data = vis_data[0, 0]
    partial = degrid_grid(own_list, own_count.reshape(1), kernel_mat, kernel_adj, gathered, own_data)
    partial = partial.reshape(chan_count, slots_count, blocks, 2, panel_rows, inner)
    inner_index = jnp.arange(inner, dtype=jnp.int32)
    outer_index = jnp.arange(outer, dtype=jnp.int32)
    cos_in, sin_in = angle_table(inner_index, inner_index, inner)
    cos_tw, sin_tw = angle_table(outer_index, inner_index, grid_width)
    cos_sel, sin_sel = angle_table(outer_index, own_list, outer)
    tw_c = cos_tw[None, :, None, None, :]
    tw_s = sin_tw[None, :, None, None, :]
    inv_c = jnp.transpose(cos_sel).astype(bf)
    inv_s = jnp.transpose(sin_sel).astype(bf)
    part_re = partial[:, :, :, 0]
    part_im = partial[:, :, :, 1]
    back_re = jnp.einsum("sa,csvrk->vacrk", inv_c, part_re, preferred_element_type=f32) - jnp.einsum(
        "sa,csvrk->vacrk", inv_s, part_im, preferred_element_type=f32
    )
    back_im = jnp.einsum("sa,csvrk->vacrk", inv_s, part_re, preferred_element_type=f32) + jnp.einsum(
        "sa,csvrk->vacrk", inv_c, part_im, preferred_element_type=f32
    )
    turned_re = (back_re * tw_c - back_im * tw_s).astype(bf)
    turned_im = (back_re * tw_s + back_im * tw_c).astype(bf)
    out_c = (cos_in * unit_scale).astype(bf)
    out_s = (sin_in * unit_scale).astype(bf)
    rows_part = jnp.einsum("vacrk,kb->vacrb", turned_re, out_c, preferred_element_type=f32) - jnp.einsum(
        "vacrk,kb->vacrb", turned_im, out_s, preferred_element_type=f32
    )
    rows_sum = lax.psum_scatter(rows_part.astype(bf), "vis", scatter_dimension=0, tiled=True)
    gradient = (
        jnp.transpose(rows_sum[0].astype(f32), (2, 1, 3, 0))
        .reshape(panel_rows, chan_count, grid_width)
    )
    upper_rim = shifted(
        wavelet_dual[panel_rows - 3 :].astype(jnp.bfloat16), ("facet", "vis"), 1
    ).astype(jnp.float32)
    padded_dual = jnp.concatenate([upper_rim, wavelet_dual], axis=0)
    synthesized = jnp.zeros_like(wavelet_dual)
    for offset in range(4):
        synthesized = (
            synthesized + high_taps[offset] * padded_dual[3 - offset : 3 - offset + panel_rows]
        )
    image_next = jnp.maximum(image - primal_step * (gradient + synthesized), 0.0)
    extrap = 2.0 * image_next - image
    lower_rim = shifted(for_sending(extrap[:3]), ("facet", "vis"), -1)
    padded_next = jnp.concatenate([extrap, lower_rim], axis=0)
    detail = jnp.zeros_like(extrap)
    for offset in range(4):
        detail = detail + high_taps[offset] * padded_next[offset : offset + panel_rows]
    update = wavelet_dual + dual_step * detail
    own_energy = jnp.sum(update * update, axis=1)
    other_energy = lax.ppermute(own_energy.astype(bf), "spec", [(0, 1), (1, 0)])
    energy = own_energy + other_energy.astype(f32)
    dual_next = update * weights[:, None, :] / jnp.maximum(weights, jnp.sqrt(energy))[:, None, :]
    return (image_next, dual_next)


def solution(mesh):
    return jax.shard_map(
        per_device,
        mesh=mesh,
        in_specs=(
            P(("facet", "vis"), "spec", None),
            P(("facet", "vis"), "spec", None),
            P(("facet", "vis"), None),
            P("facet", "vis", None, None, None),
            P("facet", "vis", "spec", None, None, None, None),
            P("facet", "vis", None),
            P("facet", "vis"),
        ),
        out_specs=(P(("facet", "vis"), "spec", None), P(("facet", "vis"), "spec", None)),
        check_vma=False,
    )
```

```python
import math

import jax
import jax.numpy as jnp
from jax import lax
from jax.sharding import PartitionSpec as P
from jax.experimental import pallas as pl
from jax.experimental.pallas import tpu as pltpu

root_three = math.sqrt(3.0)
norm_factor = 4.0 * math.sqrt(2.0)
low_taps = [
    (1.0 + root_three) / norm_factor,
    (3.0 + root_three) / norm_factor,
    (3.0 - root_three) / norm_factor,
    (1.0 - root_three) / norm_factor,
]
high_taps = [low_taps[3], -low_taps[2], low_taps[1], -low_taps[0]]
primal_step = 0.2
dual_step = 0.5
tile_width = 128
highest = lax.Precision.HIGHEST


def shifted(value, axis, steps):
    count = lax.axis_size(axis)
    initial, last = (max(0, -steps), min(count, count - steps))
    return lax.ppermute(value, axis, [(source, source + steps) for source in range(initial, last)])


def for_sending(x):

    def short(part):
        return part.astype(jnp.bfloat16) if part.dtype == jnp.float32 else part

    return jax.tree.map(short, x)


def phase_table(rows_count, cols_count, modulus):
    rows_index = jnp.arange(rows_count, dtype=jnp.int32)
    cols_index = jnp.arange(cols_count, dtype=jnp.int32)
    angle = (rows_index[:, None] * cols_index[None, :] % modulus).astype(jnp.float32) * (
        2.0 * math.pi / modulus
    )
    return (jnp.cos(angle), jnp.sin(angle))


def across_outer(values, table):
    return jnp.einsum(
        "qab,ak->qkb", values, table, precision=highest, preferred_element_type=jnp.float32
    )


def along_inner(values, table):
    return jnp.einsum(
        "qkb,bj->qkj", values, table, precision=highest, preferred_element_type=jnp.float32
    )


def fourier_rows(real_part, imag_part, sign):
    rows_count, length = real_part.shape
    outer = length // tile_width
    cos_outer, sin_outer = phase_table(outer, outer, outer)
    cos_twist, sin_twist = phase_table(outer, tile_width, length)
    cos_inner, sin_inner = phase_table(tile_width, tile_width, tile_width)
    first_re = real_part.reshape(rows_count, outer, tile_width)
    first_im = imag_part.reshape(rows_count, outer, tile_width)
    section_re = across_outer(first_re, cos_outer) - sign * across_outer(first_im, sin_outer)
    section_im = across_outer(first_im, cos_outer) + sign * across_outer(first_re, sin_outer)
    twist_re = section_re * cos_twist - sign * section_im * sin_twist
    twist_im = section_im * cos_twist + sign * section_re * sin_twist
    final_re = along_inner(twist_re, cos_inner) - sign * along_inner(twist_im, sin_inner)
    final_im = along_inner(twist_im, cos_inner) + sign * along_inner(twist_re, sin_inner)
    unit_scale = 1.0 / math.sqrt(length)
    final_re = jnp.swapaxes(final_re, 1, 2).reshape(rows_count, length) * unit_scale
    final_im = jnp.swapaxes(final_im, 1, 2).reshape(rows_count, length) * unit_scale
    return (final_re, final_im)


def kernel_blocks(kernel_pair):
    real_k = kernel_pair[0]
    imag_k = kernel_pair[1]
    top_row = jnp.stack([real_k, -imag_k], axis=1)
    bottom_row = jnp.stack([imag_k, real_k], axis=1)
    return jnp.stack([top_row, bottom_row], axis=0)


def angle_table(first, second, modulus):
    angle = ((first[:, None] * second[None, :]) % modulus).astype(jnp.float32) * (
        2.0 * math.pi / modulus
    )
    return (jnp.cos(angle), jnp.sin(angle))


def precise(spec, left, right):
    return jnp.einsum(
        spec, left, right, precision=lax.Precision.HIGH, preferred_element_type=jnp.float32
    )


def split_table(spec, values, table):
    high = table.astype(jnp.bfloat16)
    low = (table - high.astype(jnp.float32)).astype(jnp.bfloat16)
    return jnp.einsum(spec, values, high, preferred_element_type=jnp.float32) + jnp.einsum(
        spec, values, low, preferred_element_type=jnp.float32
    )


def degrid_body(list_ref, count_ref, kmat_ref, kadj_ref, *refs):
    tile_refs, vis_ref, out_ref = refs[:-2], refs[-2], refs[-1]
    group = len(tile_refs)
    step = pl.program_id(1)
    for place, grid_ref in enumerate(tile_refs):
        slot = step * group + place

        @pl.when(slot < count_ref[0])
        def _():
            rows = grid_ref.shape[0] * grid_ref.shape[1] * grid_ref.shape[2]
            tile = grid_ref[...].astype(jnp.float32).reshape(rows, grid_ref.shape[3]).astype(jnp.bfloat16)
            predicted = jnp.dot(kmat_ref[...], tile, preferred_element_type=jnp.float32)
            measured = vis_ref[:, place].astype(jnp.float32).reshape(predicted.shape)
            residual = (predicted - measured).astype(jnp.bfloat16)
            gridded = jnp.dot(kadj_ref[...], residual, preferred_element_type=jnp.float32)
            out_ref[place] = gridded.astype(out_ref.dtype)

        @pl.when(slot >= count_ref[0])
        def _():
            out_ref[place] = jnp.zeros(out_ref.shape[1:], out_ref.dtype)


def tile_spec(blocks, parts, rows, inner, group, place):
    return pl.BlockSpec(
        (blocks, None, parts, rows, inner),
        lambda c, s, lst, cnt: (0, c, 0, 0, lst[s * group + place]),
    )


def degrid_grid(own_list, own_count, kernel_mat, kernel_adj, gathered, own_data):
    blocks, chans, parts, rows, width = gathered.shape
    slots = own_list.shape[0]
    group = 8
    out_rows, in_rows = kernel_mat.shape
    inner = tile_width
    flops = 4 * out_rows * in_rows * inner * chans * slots
    return pl.pallas_call(
        degrid_body,
        grid_spec=pltpu.PrefetchScalarGridSpec(
            num_scalar_prefetch=2,
            grid=(chans, slots // group),
            in_specs=[
                pl.BlockSpec((out_rows, in_rows), lambda c, s, lst, cnt: (0, 0)),
                pl.BlockSpec((in_rows, out_rows), lambda c, s, lst, cnt: (0, 0)),
            ]
            + [tile_spec(blocks, parts, rows, inner, group, place) for place in range(group)]
            + [
                pl.BlockSpec(
                    (None, parts, group, out_rows // parts, inner),
                    lambda c, s, lst, cnt: (c, 0, s, 0, 0),
                ),
            ],
            out_specs=pl.BlockSpec((None, group, in_rows, inner), lambda c, s, lst, cnt: (c, s, 0, 0)),
        ),
        out_shape=jax.ShapeDtypeStruct((chans, slots, in_rows, inner), jnp.bfloat16),
        cost_estimate=pl.CostEstimate(
            flops=flops, bytes_accessed=2 * chans * slots * (out_rows + 2 * in_rows) * inner,
            transcendentals=0,
        ),
    )(own_list, own_count, kernel_mat, kernel_adj, *([gathered] * group), own_data)


def per_device(image, wavelet_dual, weights, kernels, vis_data, tile_list, tile_count):
    panel_rows, chan_count, grid_width = image.shape
    inner = tile_width
    outer = grid_width // inner
    unit_scale = 1.0 / math.sqrt(grid_width)
    bf = jnp.bfloat16
    f32 = jnp.float32
    own_list = tile_list[0, 0]
    own_count = tile_count[0, 0]
    slots_count = own_list.shape[0]
    image_rows = image.reshape(panel_rows * chan_count, grid_width)
    grid_re, grid_im = fourier_rows(image_rows, jnp.zeros_like(image_rows), -1.0)
    grid_panel = (
        jnp.stack([grid_re, grid_im], axis=1)
        .reshape(panel_rows, chan_count, 2, grid_width)
        .astype(bf)
    )
    panel_t = jnp.transpose(grid_panel, (1, 2, 0, 3))
    gathered = lax.all_gather(panel_t, "vis", axis=0)
    blocks = gathered.shape[0]
    stacked = kernel_blocks(kernels[0, 0])
    out_rows, vis_rows = stacked.shape[0] * stacked.shape[1], stacked.shape[2] * blocks * panel_rows
    kernel_mat = jnp.transpose(
        stacked.reshape(2, -1, 2, blocks, panel_rows), (0, 1, 3, 2, 4)
    ).reshape(out_rows, vis_rows)
    kernel_adj = jnp.transpose(kernel_mat)
    own_data = vis_data[0, 0]
    partial = degrid_grid(own_list, own_count.reshape(1), kernel_mat, kernel_adj, gathered, own_data)
    partial = partial.reshape(chan_count, slots_count, blocks, 2, panel_rows, inner)
    inner_index = jnp.arange(inner, dtype=jnp.int32)
    outer_index = jnp.arange(outer, dtype=jnp.int32)
    cos_in, sin_in = angle_table(inner_index, inner_index, inner)
    cos_tw, sin_tw = angle_table(outer_index, inner_index, grid_width)
    cos_sel, sin_sel = angle_table(outer_index, own_list, outer)
    tw_c = cos_tw[None, :, None, None, :]
    tw_s = sin_tw[None, :, None, None, :]
    inv_c = jnp.transpose(cos_sel).astype(bf)
    inv_s = jnp.transpose(sin_sel).astype(bf)
    part_re = partial[:, :, :, 0]
    part_im = partial[:, :, :, 1]
    back_re = jnp.einsum("sa,csvrk->vacrk", inv_c, part_re, preferred_element_type=f32) - jnp.einsum(
        "sa,csvrk->vacrk", inv_s, part_im, preferred_element_type=f32
    )
    back_im = jnp.einsum("sa,csvrk->vacrk", inv_s, part_re, preferred_element_type=f32) + jnp.einsum(
        "sa,csvrk->vacrk", inv_c, part_im, preferred_element_type=f32
    )
    turned_re = (back_re * tw_c - back_im * tw_s).astype(bf)
    turned_im = (back_re * tw_s + back_im * tw_c).astype(bf)
    out_c = (cos_in * unit_scale).astype(bf)
    out_s = (sin_in * unit_scale).astype(bf)
    rows_part = jnp.einsum("vacrk,kb->vacrb", turned_re, out_c, preferred_element_type=f32) - jnp.einsum(
        "vacrk,kb->vacrb", turned_im, out_s, preferred_element_type=f32
    )
    rows_sum = lax.psum_scatter(rows_part.astype(bf), "vis", scatter_dimension=0, tiled=True)
    gradient = (
        jnp.transpose(rows_sum[0].astype(f32), (2, 1, 3, 0))
        .reshape(panel_rows, chan_count, grid_width)
    )
    upper_rim = shifted(
        wavelet_dual[panel_rows - 3 :].astype(jnp.bfloat16), ("facet", "vis"), 1
    ).astype(jnp.float32)
    padded_dual = jnp.concatenate([upper_rim, wavelet_dual], axis=0)
    synthesized = jnp.zeros_like(wavelet_dual)
    for offset in range(4):
        synthesized = (
            synthesized + high_taps[offset] * padded_dual[3 - offset : 3 - offset + panel_rows]
        )
    image_next = jnp.maximum(image - primal_step * (gradient + synthesized), 0.0)
    extrap = 2.0 * image_next - image
    lower_rim = shifted(for_sending(extrap[:3]), ("facet", "vis"), -1)
    padded_next = jnp.concatenate([extrap, lower_rim], axis=0)
    detail = jnp.zeros_like(extrap)
    for offset in range(4):
        detail = detail + high_taps[offset] * padded_next[offset : offset + panel_rows]
    update = wavelet_dual + dual_step * detail
    own_energy = jnp.sum(update * update, axis=1)
    other_energy = lax.ppermute(own_energy.astype(bf), "spec", [(0, 1), (1, 0)])
    energy = own_energy + other_energy.astype(f32)
    dual_next = update * weights[:, None, :] / jnp.maximum(weights, jnp.sqrt(energy))[:, None, :]
    return (image_next, dual_next)


def solution(mesh):
    return jax.shard_map(
        per_device,
        mesh=mesh,
        in_specs=(
            P(("facet", "vis"), "spec", None),
            P(("facet", "vis"), "spec", None),
            P(("facet", "vis"), None),
            P("facet", "vis", None, None, None),
            P("facet", "vis", "spec", None, None, None, None),
            P("facet", "vis", None),
            P("facet", "vis"),
        ),
        out_specs=(P(("facet", "vis"), "spec", None), P(("facet", "vis"), "spec", None)),
        check_vma=False,
    )
```

```python
import math

import jax
import jax.numpy as jnp
from jax import lax
from jax.sharding import PartitionSpec as P
from jax.experimental import pallas as pl
from jax.experimental.pallas import tpu as pltpu

root_three = math.sqrt(3.0)
norm_factor = 4.0 * math.sqrt(2.0)
low_taps = [
    (1.0 + root_three) / norm_factor,
    (3.0 + root_three) / norm_factor,
    (3.0 - root_three) / norm_factor,
    (1.0 - root_three) / norm_factor,
]
high_taps = [low_taps[3], -low_taps[2], low_taps[1], -low_taps[0]]
primal_step = 0.2
dual_step = 0.5
tile_width = 128
highest = lax.Precision.HIGHEST


def shifted(value, axis, steps):
    count = lax.axis_size(axis)
    initial, last = (max(0, -steps), min(count, count - steps))
    return lax.ppermute(value, axis, [(source, source + steps) for source in range(initial, last)])


def for_sending(x):

    def short(part):
        return part.astype(jnp.bfloat16) if part.dtype == jnp.float32 else part

    return jax.tree.map(short, x)


def phase_table(rows_count, cols_count, modulus):
    rows_index = jnp.arange(rows_count, dtype=jnp.int32)
    cols_index = jnp.arange(cols_count, dtype=jnp.int32)
    angle = (rows_index[:, None] * cols_index[None, :] % modulus).astype(jnp.float32) * (
        2.0 * math.pi / modulus
    )
    return (jnp.cos(angle), jnp.sin(angle))


def across_outer(values, table):
    return jnp.einsum(
        "qab,ak->qkb", values, table, precision=highest, preferred_element_type=jnp.float32
    )


def along_inner(values, table):
    return jnp.einsum(
        "qkb,bj->qkj", values, table, precision=highest, preferred_element_type=jnp.float32
    )


def fourier_rows(real_part, imag_part, sign):
    rows_count, length = real_part.shape
    outer = length // tile_width
    cos_outer, sin_outer = phase_table(outer, outer, outer)
    cos_twist, sin_twist = phase_table(outer, tile_width, length)
    cos_inner, sin_inner = phase_table(tile_width, tile_width, tile_width)
    first_re = real_part.reshape(rows_count, outer, tile_width)
    first_im = imag_part.reshape(rows_count, outer, tile_width)
    section_re = across_outer(first_re, cos_outer) - sign * across_outer(first_im, sin_outer)
    section_im = across_outer(first_im, cos_outer) + sign * across_outer(first_re, sin_outer)
    twist_re = section_re * cos_twist - sign * section_im * sin_twist
    twist_im = section_im * cos_twist + sign * section_re * sin_twist
    final_re = along_inner(twist_re, cos_inner) - sign * along_inner(twist_im, sin_inner)
    final_im = along_inner(twist_im, cos_inner) + sign * along_inner(twist_re, sin_inner)
    unit_scale = 1.0 / math.sqrt(length)
    final_re = jnp.swapaxes(final_re, 1, 2).reshape(rows_count, length) * unit_scale
    final_im = jnp.swapaxes(final_im, 1, 2).reshape(rows_count, length) * unit_scale
    return (final_re, final_im)


def kernel_blocks(kernel_pair):
    real_k = kernel_pair[0]
    imag_k = kernel_pair[1]
    top_row = jnp.stack([real_k, -imag_k], axis=1)
    bottom_row = jnp.stack([imag_k, real_k], axis=1)
    return jnp.stack([top_row, bottom_row], axis=0)


def angle_table(first, second, modulus):
    angle = ((first[:, None] * second[None, :]) % modulus).astype(jnp.float32) * (
        2.0 * math.pi / modulus
    )
    return (jnp.cos(angle), jnp.sin(angle))


def precise(spec, left, right):
    return jnp.einsum(
        spec, left, right, precision=lax.Precision.HIGH, preferred_element_type=jnp.float32
    )


def split_table(spec, values, table):
    high = table.astype(jnp.bfloat16)
    low = (table - high.astype(jnp.float32)).astype(jnp.bfloat16)
    return jnp.einsum(spec, values, high, preferred_element_type=jnp.float32) + jnp.einsum(
        spec, values, low, preferred_element_type=jnp.float32
    )


def degrid_body(list_ref, count_ref, kmat_ref, kadj_ref, *refs):
    tile_refs, vis_ref, out_ref = refs[:-2], refs[-2], refs[-1]
    group = len(tile_refs)
    step = pl.program_id(1)
    for place, grid_ref in enumerate(tile_refs):
        slot = step * group + place

        @pl.when(slot < count_ref[0])
        def _():
            rows = grid_ref.shape[0] * grid_ref.shape[1] * grid_ref.shape[2]
            tile = grid_ref[...].astype(jnp.float32).reshape(rows, grid_ref.shape[3]).astype(jnp.bfloat16)
            predicted = jnp.dot(kmat_ref[...], tile, preferred_element_type=jnp.float32)
            measured = vis_ref[:, place].astype(jnp.float32).reshape(predicted.shape)
            residual = (predicted - measured).astype(jnp.bfloat16)
            gridded = jnp.dot(kadj_ref[...], residual, preferred_element_type=jnp.float32)
            out_ref[place] = gridded.astype(out_ref.dtype)

        @pl.when(slot >= count_ref[0])
        def _():
            out_ref[place] = jnp.zeros(out_ref.shape[1:], out_ref.dtype)


def tile_spec(blocks, parts, rows, inner, group, place):
    return pl.BlockSpec(
        (blocks, None, parts, rows, inner),
        lambda c, s, lst, cnt: (0, c, 0, 0, lst[s * group + place]),
    )


def degrid_grid(own_list, own_count, kernel_mat, kernel_adj, gathered, own_data):
    blocks, chans, parts, rows, width = gathered.shape
    slots = own_list.shape[0]
    group = 4
    out_rows, in_rows = kernel_mat.shape
    inner = tile_width
    flops = 4 * out_rows * in_rows * inner * chans * slots
    return pl.pallas_call(
        degrid_body,
        grid_spec=pltpu.PrefetchScalarGridSpec(
            num_scalar_prefetch=2,
            grid=(chans, slots // group),
            in_specs=[
                pl.BlockSpec((out_rows, in_rows), lambda c, s, lst, cnt: (0, 0)),
                pl.BlockSpec((in_rows, out_rows), lambda c, s, lst, cnt: (0, 0)),
            ]
            + [tile_spec(blocks, parts, rows, inner, group, place) for place in range(group)]
            + [
                pl.BlockSpec(
                    (None, parts, group, out_rows // parts, inner),
                    lambda c, s, lst, cnt: (c, 0, s, 0, 0),
                ),
            ],
            out_specs=pl.BlockSpec((None, group, in_rows, inner), lambda c, s, lst, cnt: (c, s, 0, 0)),
        ),
        out_shape=jax.ShapeDtypeStruct((chans, slots, in_rows, inner), jnp.bfloat16),
        cost_estimate=pl.CostEstimate(
            flops=flops, bytes_accessed=2 * chans * slots * (out_rows + 2 * in_rows) * inner,
            transcendentals=0,
        ),
    )(own_list, own_count, kernel_mat, kernel_adj, *([gathered] * group), own_data)


def per_device(image, wavelet_dual, weights, kernels, vis_data, tile_list, tile_count):
    panel_rows, chan_count, grid_width = image.shape
    inner = tile_width
    outer = grid_width // inner
    unit_scale = 1.0 / math.sqrt(grid_width)
    bf = jnp.bfloat16
    f32 = jnp.float32
    own_list = tile_list[0, 0]
    own_count = tile_count[0, 0]
    slots_count = own_list.shape[0]
    image_rows = image.reshape(panel_rows * chan_count, grid_width)
    grid_re, grid_im = fourier_rows(image_rows, jnp.zeros_like(image_rows), -1.0)
    grid_panel = (
        jnp.stack([grid_re, grid_im], axis=1)
        .reshape(panel_rows, chan_count, 2, grid_width)
        .astype(bf)
    )
    panel_t = jnp.transpose(grid_panel, (1, 2, 0, 3))
    gathered = lax.all_gather(panel_t, "vis", axis=0)
    blocks = gathered.shape[0]
    stacked = kernel_blocks(kernels[0, 0])
    out_rows, vis_rows = stacked.shape[0] * stacked.shape[1], stacked.shape[2] * blocks * panel_rows
    kernel_mat = jnp.transpose(
        stacked.reshape(2, -1, 2, blocks, panel_rows), (0, 1, 3, 2, 4)
    ).reshape(out_rows, vis_rows)
    kernel_adj = jnp.transpose(kernel_mat)
    own_data = vis_data[0, 0]
    partial = degrid_grid(own_list, own_count.reshape(1), kernel_mat, kernel_adj, gathered, own_data)
    partial = partial.reshape(chan_count, slots_count, blocks, 2, panel_rows, inner)
    inner_index = jnp.arange(inner, dtype=jnp.int32)
    outer_index = jnp.arange(outer, dtype=jnp.int32)
    cos_in, sin_in = angle_table(inner_index, inner_index, inner)
    cos_tw, sin_tw = angle_table(outer_index, inner_index, grid_width)
    cos_sel, sin_sel = angle_table(outer_index, own_list, outer)
    tw_c = cos_tw[None, :, None, None, :]
    tw_s = sin_tw[None, :, None, None, :]
    inv_c = jnp.transpose(cos_sel).astype(bf)
    inv_s = jnp.transpose(sin_sel).astype(bf)
    inverse_mat = jnp.stack([jnp.stack([inv_c, -inv_s]), jnp.stack([inv_s, inv_c])])
    back = jnp.einsum(
        "jisa,csvirk->jvacrk", inverse_mat, partial, preferred_element_type=f32
    ).astype(bf)
    back_re = back[0].astype(f32)
    back_im = back[1].astype(f32)
    turned_re = (back_re * tw_c - back_im * tw_s).astype(bf)
    turned_im = (back_re * tw_s + back_im * tw_c).astype(bf)
    out_c = (cos_in * unit_scale).astype(bf)
    out_s = (sin_in * unit_scale).astype(bf)
    rows_part = jnp.einsum("vacrk,kb->vacrb", turned_re, out_c, preferred_element_type=f32) - jnp.einsum(
        "vacrk,kb->vacrb", turned_im, out_s, preferred_element_type=f32
    )
    rows_sum = lax.psum_scatter(rows_part.astype(bf), "vis", scatter_dimension=0, tiled=True)
    gradient = (
        jnp.transpose(rows_sum[0].astype(f32), (2, 1, 3, 0))
        .reshape(panel_rows, chan_count, grid_width)
    )
    upper_rim = shifted(
        wavelet_dual[panel_rows - 3 :].astype(jnp.bfloat16), ("facet", "vis"), 1
    ).astype(jnp.float32)
    padded_dual = jnp.concatenate([upper_rim, wavelet_dual], axis=0)
    synthesized = jnp.zeros_like(wavelet_dual)
    for offset in range(4):
        synthesized = (
            synthesized + high_taps[offset] * padded_dual[3 - offset : 3 - offset + panel_rows]
        )
    image_next = jnp.maximum(image - primal_step * (gradient + synthesized), 0.0)
    extrap = 2.0 * image_next - image
    lower_rim = shifted(for_sending(extrap[:3]), ("facet", "vis"), -1)
    padded_next = jnp.concatenate([extrap, lower_rim], axis=0)
    detail = jnp.zeros_like(extrap)
    for offset in range(4):
        detail = detail + high_taps[offset] * padded_next[offset : offset + panel_rows]
    update = wavelet_dual + dual_step * detail
    own_energy = jnp.sum(update * update, axis=1)
    other_energy = lax.ppermute(own_energy.astype(bf), "spec", [(0, 1), (1, 0)])
    energy = own_energy + other_energy.astype(f32)
    dual_next = update * weights[:, None, :] / jnp.maximum(weights, jnp.sqrt(energy))[:, None, :]
    return (image_next, dual_next)


def solution(mesh):
    return jax.shard_map(
        per_device,
        mesh=mesh,
        in_specs=(
            P(("facet", "vis"), "spec", None),
            P(("facet", "vis"), "spec", None),
            P(("facet", "vis"), None),
            P("facet", "vis", None, None, None),
            P("facet", "vis", "spec", None, None, None, None),
            P("facet", "vis", None),
            P("facet", "vis"),
        ),
        out_specs=(P(("facet", "vis"), "spec", None), P(("facet", "vis"), "spec", None)),
        check_vma=False,
    )
```

```python
import math

import jax
import jax.numpy as jnp
from jax import lax
from jax.sharding import PartitionSpec as P
from jax.experimental import pallas as pl
from jax.experimental.pallas import tpu as pltpu

root_three = math.sqrt(3.0)
norm_factor = 4.0 * math.sqrt(2.0)
low_taps = [
    (1.0 + root_three) / norm_factor,
    (3.0 + root_three) / norm_factor,
    (3.0 - root_three) / norm_factor,
    (1.0 - root_three) / norm_factor,
]
high_taps = [low_taps[3], -low_taps[2], low_taps[1], -low_taps[0]]
primal_step = 0.2
dual_step = 0.5
tile_width = 128
highest = lax.Precision.HIGHEST


def shifted(value, axis, steps):
    count = lax.axis_size(axis)
    initial, last = (max(0, -steps), min(count, count - steps))
    return lax.ppermute(value, axis, [(source, source + steps) for source in range(initial, last)])


def for_sending(x):

    def short(part):
        return part.astype(jnp.bfloat16) if part.dtype == jnp.float32 else part

    return jax.tree.map(short, x)


def phase_table(rows_count, cols_count, modulus):
    rows_index = jnp.arange(rows_count, dtype=jnp.int32)
    cols_index = jnp.arange(cols_count, dtype=jnp.int32)
    angle = (rows_index[:, None] * cols_index[None, :] % modulus).astype(jnp.float32) * (
        2.0 * math.pi / modulus
    )
    return (jnp.cos(angle), jnp.sin(angle))


def across_outer(values, table):
    return jnp.einsum(
        "qab,ak->qkb", values, table, precision=highest, preferred_element_type=jnp.float32
    )


def along_inner(values, table):
    return jnp.einsum(
        "qkb,bj->qkj", values, table, precision=highest, preferred_element_type=jnp.float32
    )


def fourier_rows(real_part, imag_part, sign):
    rows_count, length = real_part.shape
    outer = length // tile_width
    cos_outer, sin_outer = phase_table(outer, outer, outer)
    cos_twist, sin_twist = phase_table(outer, tile_width, length)
    cos_inner, sin_inner = phase_table(tile_width, tile_width, tile_width)
    first_re = real_part.reshape(rows_count, outer, tile_width)
    first_im = imag_part.reshape(rows_count, outer, tile_width)
    section_re = across_outer(first_re, cos_outer) - sign * across_outer(first_im, sin_outer)
    section_im = across_outer(first_im, cos_outer) + sign * across_outer(first_re, sin_outer)
    twist_re = section_re * cos_twist - sign * section_im * sin_twist
    twist_im = section_im * cos_twist + sign * section_re * sin_twist
    final_re = along_inner(twist_re, cos_inner) - sign * along_inner(twist_im, sin_inner)
    final_im = along_inner(twist_im, cos_inner) + sign * along_inner(twist_re, sin_inner)
    unit_scale = 1.0 / math.sqrt(length)
    final_re = jnp.swapaxes(final_re, 1, 2).reshape(rows_count, length) * unit_scale
    final_im = jnp.swapaxes(final_im, 1, 2).reshape(rows_count, length) * unit_scale
    return (final_re, final_im)


def kernel_blocks(kernel_pair):
    real_k = kernel_pair[0]
    imag_k = kernel_pair[1]
    top_row = jnp.stack([real_k, -imag_k], axis=1)
    bottom_row = jnp.stack([imag_k, real_k], axis=1)
    return jnp.stack([top_row, bottom_row], axis=0)


def angle_table(first, second, modulus):
    angle = ((first[:, None] * second[None, :]) % modulus).astype(jnp.float32) * (
        2.0 * math.pi / modulus
    )
    return (jnp.cos(angle), jnp.sin(angle))


def precise(spec, left, right):
    return jnp.einsum(
        spec, left, right, precision=lax.Precision.HIGH, preferred_element_type=jnp.float32
    )


def split_table(spec, values, table):
    high = table.astype(jnp.bfloat16)
    low = (table - high.astype(jnp.float32)).astype(jnp.bfloat16)
    return jnp.einsum(spec, values, high, preferred_element_type=jnp.float32) + jnp.einsum(
        spec, values, low, preferred_element_type=jnp.float32
    )


def degrid_body(list_ref, count_ref, kmat_ref, kadj_ref, *refs):
    tile_refs, vis_ref, out_ref = refs[:-2], refs[-2], refs[-1]
    group = len(tile_refs)
    step = pl.program_id(1)
    for place, grid_ref in enumerate(tile_refs):
        slot = step * group + place

        @pl.when(slot < count_ref[0])
        def _():
            rows = grid_ref.shape[0] * grid_ref.shape[1] * grid_ref.shape[2]
            tile = grid_ref[...].astype(jnp.float32).reshape(rows, grid_ref.shape[3]).astype(jnp.bfloat16)
            predicted = jnp.dot(kmat_ref[...], tile, preferred_element_type=jnp.float32)
            measured = vis_ref[:, place].astype(jnp.float32).reshape(predicted.shape)
            residual = (predicted - measured).astype(jnp.bfloat16)
            gridded = jnp.dot(kadj_ref[...], residual, preferred_element_type=jnp.float32)
            out_ref[place] = gridded.astype(out_ref.dtype)

        @pl.when(slot >= count_ref[0])
        def _():
            out_ref[place] = jnp.zeros(out_ref.shape[1:], out_ref.dtype)


def tile_spec(blocks, parts, rows, inner, group, place):
    return pl.BlockSpec(
        (blocks, None, parts, rows, inner),
        lambda c, s, lst, cnt: (0, c, 0, 0, lst[s * group + place]),
    )


def degrid_grid(own_list, own_count, kernel_mat, kernel_adj, gathered, own_data):
    blocks, chans, parts, rows, width = gathered.shape
    slots = own_list.shape[0]
    group = 4
    out_rows, in_rows = kernel_mat.shape
    inner = tile_width
    flops = 4 * out_rows * in_rows * inner * chans * slots
    return pl.pallas_call(
        degrid_body,
        grid_spec=pltpu.PrefetchScalarGridSpec(
            num_scalar_prefetch=2,
            grid=(chans, slots // group),
            in_specs=[
                pl.BlockSpec((out_rows, in_rows), lambda c, s, lst, cnt: (0, 0)),
                pl.BlockSpec((in_rows, out_rows), lambda c, s, lst, cnt: (0, 0)),
            ]
            + [tile_spec(blocks, parts, rows, inner, group, place) for place in range(group)]
            + [
                pl.BlockSpec(
                    (None, parts, group, out_rows // parts, inner),
                    lambda c, s, lst, cnt: (c, 0, s, 0, 0),
                ),
            ],
            out_specs=pl.BlockSpec((None, group, in_rows, inner), lambda c, s, lst, cnt: (c, s, 0, 0)),
        ),
        out_shape=jax.ShapeDtypeStruct((chans, slots, in_rows, inner), jnp.bfloat16),
        cost_estimate=pl.CostEstimate(
            flops=flops, bytes_accessed=2 * chans * slots * (out_rows + 2 * in_rows) * inner,
            transcendentals=0,
        ),
    )(own_list, own_count, kernel_mat, kernel_adj, *([gathered] * group), own_data)


def per_device(image, wavelet_dual, weights, kernels, vis_data, tile_list, tile_count):
    panel_rows, chan_count, grid_width = image.shape
    inner = tile_width
    outer = grid_width // inner
    unit_scale = 1.0 / math.sqrt(grid_width)
    bf = jnp.bfloat16
    f32 = jnp.float32
    own_list = tile_list[0, 0]
    own_count = tile_count[0, 0]
    slots_count = own_list.shape[0]
    image_rows = image.reshape(panel_rows * chan_count, grid_width)
    grid_re, grid_im = fourier_rows(image_rows, jnp.zeros_like(image_rows), -1.0)
    grid_panel = (
        jnp.stack([grid_re, grid_im], axis=1)
        .reshape(panel_rows, chan_count, 2, grid_width)
        .astype(bf)
    )
    panel_t = jnp.transpose(grid_panel, (1, 2, 0, 3))
    gathered = lax.all_gather(panel_t, "vis", axis=0)
    blocks = gathered.shape[0]
    stacked = kernel_blocks(kernels[0, 0])
    out_rows, vis_rows = stacked.shape[0] * stacked.shape[1], stacked.shape[2] * blocks * panel_rows
    kernel_mat = jnp.transpose(
        stacked.reshape(2, -1, 2, blocks, panel_rows), (0, 1, 3, 2, 4)
    ).reshape(out_rows, vis_rows)
    kernel_adj = jnp.transpose(kernel_mat)
    own_data = vis_data[0, 0]
    partial = degrid_grid(own_list, own_count.reshape(1), kernel_mat, kernel_adj, gathered, own_data)
    partial = partial.reshape(chan_count, slots_count, blocks, 2, panel_rows, inner)
    inner_index = jnp.arange(inner, dtype=jnp.int32)
    outer_index = jnp.arange(outer, dtype=jnp.int32)
    cos_in, sin_in = angle_table(inner_index, inner_index, inner)
    cos_tw, sin_tw = angle_table(outer_index, inner_index, grid_width)
    cos_sel, sin_sel = angle_table(outer_index, own_list, outer)
    tw_c = cos_tw[None, :, None, None, :]
    tw_s = sin_tw[None, :, None, None, :]
    inv_c = jnp.transpose(cos_sel).astype(bf)
    inv_s = jnp.transpose(sin_sel).astype(bf)
    inverse_mat = jnp.stack([jnp.stack([inv_c, -inv_s]), jnp.stack([inv_s, inv_c])])
    back = jnp.einsum(
        "jisa,csvirk->jvacrk", inverse_mat, partial, preferred_element_type=f32
    ).astype(bf)
    back_re = back[0].astype(f32)
    back_im = back[1].astype(f32)
    turned = jnp.stack(
        [back_re * tw_c - back_im * tw_s, back_re * tw_s + back_im * tw_c]
    ).astype(bf)
    out_table = jnp.stack([cos_in * unit_scale, -sin_in * unit_scale]).astype(bf)
    rows_part = jnp.einsum(
        "jvacrk,jkb->vacrb", turned, out_table, preferred_element_type=f32
    ).astype(bf)
    rows_sum = lax.psum_scatter(rows_part, "vis", scatter_dimension=0, tiled=True)
    gradient = (
        jnp.transpose(rows_sum[0].astype(f32), (2, 1, 3, 0))
        .reshape(panel_rows, chan_count, grid_width)
    )
    upper_rim = shifted(
        wavelet_dual[panel_rows - 3 :].astype(jnp.bfloat16), ("facet", "vis"), 1
    ).astype(jnp.float32)
    padded_dual = jnp.concatenate([upper_rim, wavelet_dual], axis=0)
    synthesized = jnp.zeros_like(wavelet_dual)
    for offset in range(4):
        synthesized = (
            synthesized + high_taps[offset] * padded_dual[3 - offset : 3 - offset + panel_rows]
        )
    image_next = jnp.maximum(image - primal_step * (gradient + synthesized), 0.0)
    extrap = 2.0 * image_next - image
    lower_rim = shifted(for_sending(extrap[:3]), ("facet", "vis"), -1)
    padded_next = jnp.concatenate([extrap, lower_rim], axis=0)
    detail = jnp.zeros_like(extrap)
    for offset in range(4):
        detail = detail + high_taps[offset] * padded_next[offset : offset + panel_rows]
    update = wavelet_dual + dual_step * detail
    own_energy = jnp.sum(update * update, axis=1)
    other_energy = lax.ppermute(own_energy.astype(bf), "spec", [(0, 1), (1, 0)])
    energy = own_energy + other_energy.astype(f32)
    dual_next = update * weights[:, None, :] / jnp.maximum(weights, jnp.sqrt(energy))[:, None, :]
    return (image_next, dual_next)


def solution(mesh):
    return jax.shard_map(
        per_device,
        mesh=mesh,
        in_specs=(
            P(("facet", "vis"), "spec", None),
            P(("facet", "vis"), "spec", None),
            P(("facet", "vis"), None),
            P("facet", "vis", None, None, None),
            P("facet", "vis", "spec", None, None, None, None),
            P("facet", "vis", None),
            P("facet", "vis"),
        ),
        out_specs=(P(("facet", "vis"), "spec", None), P(("facet", "vis"), "spec", None)),
        check_vma=False,
    )
```

```python
import math

import jax
import jax.numpy as jnp
from jax import lax
from jax.sharding import PartitionSpec as P
from jax.experimental import pallas as pl
from jax.experimental.pallas import tpu as pltpu

root_three = math.sqrt(3.0)
norm_factor = 4.0 * math.sqrt(2.0)
low_taps = [
    (1.0 + root_three) / norm_factor,
    (3.0 + root_three) / norm_factor,
    (3.0 - root_three) / norm_factor,
    (1.0 - root_three) / norm_factor,
]
high_taps = [low_taps[3], -low_taps[2], low_taps[1], -low_taps[0]]
primal_step = 0.2
dual_step = 0.5
tile_width = 128
highest = lax.Precision.HIGH


def shifted(value, axis, steps):
    count = lax.axis_size(axis)
    initial, last = (max(0, -steps), min(count, count - steps))
    return lax.ppermute(value, axis, [(source, source + steps) for source in range(initial, last)])


def for_sending(x):

    def short(part):
        return part.astype(jnp.bfloat16) if part.dtype == jnp.float32 else part

    return jax.tree.map(short, x)


def phase_table(rows_count, cols_count, modulus):
    rows_index = jnp.arange(rows_count, dtype=jnp.int32)
    cols_index = jnp.arange(cols_count, dtype=jnp.int32)
    angle = (rows_index[:, None] * cols_index[None, :] % modulus).astype(jnp.float32) * (
        2.0 * math.pi / modulus
    )
    return (jnp.cos(angle), jnp.sin(angle))


def across_outer(values, table):
    return jnp.einsum(
        "qab,ak->qkb", values, table, precision=highest, preferred_element_type=jnp.float32
    )


def along_inner(values, table):
    return jnp.einsum(
        "qkb,bj->qkj", values, table, precision=highest, preferred_element_type=jnp.float32
    )


def fourier_rows(real_part, imag_part, sign):
    rows_count, length = real_part.shape
    outer = length // tile_width
    cos_outer, sin_outer = phase_table(outer, outer, outer)
    cos_twist, sin_twist = phase_table(outer, tile_width, length)
    cos_inner, sin_inner = phase_table(tile_width, tile_width, tile_width)
    first_re = real_part.reshape(rows_count, outer, tile_width)
    first_im = imag_part.reshape(rows_count, outer, tile_width)
    section_re = across_outer(first_re, cos_outer) - sign * across_outer(first_im, sin_outer)
    section_im = across_outer(first_im, cos_outer) + sign * across_outer(first_re, sin_outer)
    twist_re = section_re * cos_twist - sign * section_im * sin_twist
    twist_im = section_im * cos_twist + sign * section_re * sin_twist
    final_re = along_inner(twist_re, cos_inner) - sign * along_inner(twist_im, sin_inner)
    final_im = along_inner(twist_im, cos_inner) + sign * along_inner(twist_re, sin_inner)
    unit_scale = 1.0 / math.sqrt(length)
    final_re = jnp.swapaxes(final_re, 1, 2).reshape(rows_count, length) * unit_scale
    final_im = jnp.swapaxes(final_im, 1, 2).reshape(rows_count, length) * unit_scale
    return (final_re, final_im)


def kernel_blocks(kernel_pair):
    real_k = kernel_pair[0]
    imag_k = kernel_pair[1]
    top_row = jnp.stack([real_k, -imag_k], axis=1)
    bottom_row = jnp.stack([imag_k, real_k], axis=1)
    return jnp.stack([top_row, bottom_row], axis=0)


def angle_table(first, second, modulus):
    angle = ((first[:, None] * second[None, :]) % modulus).astype(jnp.float32) * (
        2.0 * math.pi / modulus
    )
    return (jnp.cos(angle), jnp.sin(angle))


def precise(spec, left, right):
    return jnp.einsum(
        spec, left, right, precision=lax.Precision.HIGH, preferred_element_type=jnp.float32
    )


def split_table(spec, values, table):
    high = table.astype(jnp.bfloat16)
    low = (table - high.astype(jnp.float32)).astype(jnp.bfloat16)
    return jnp.einsum(spec, values, high, preferred_element_type=jnp.float32) + jnp.einsum(
        spec, values, low, preferred_element_type=jnp.float32
    )


def degrid_body(list_ref, count_ref, kmat_ref, kadj_ref, *refs):
    tile_refs, vis_ref, out_ref = refs[:-2], refs[-2], refs[-1]
    group = len(tile_refs)
    step = pl.program_id(1)
    for place, grid_ref in enumerate(tile_refs):
        slot = step * group + place

        @pl.when(slot < count_ref[0])
        def _():
            rows = grid_ref.shape[0] * grid_ref.shape[1] * grid_ref.shape[2]
            tile = grid_ref[...].astype(jnp.float32).reshape(rows, grid_ref.shape[3]).astype(jnp.bfloat16)
            predicted = jnp.dot(kmat_ref[...], tile, preferred_element_type=jnp.float32)
            measured = vis_ref[:, place].astype(jnp.float32).reshape(predicted.shape)
            residual = (predicted - measured).astype(jnp.bfloat16)
            gridded = jnp.dot(kadj_ref[...], residual, preferred_element_type=jnp.float32)
            out_ref[place] = gridded.astype(out_ref.dtype)

        @pl.when(slot >= count_ref[0])
        def _():
            out_ref[place] = jnp.zeros(out_ref.shape[1:], out_ref.dtype)


def tile_spec(blocks, parts, rows, inner, group, place):
    return pl.BlockSpec(
        (blocks, None, parts, rows, inner),
        lambda c, s, lst, cnt: (0, c, 0, 0, lst[s * group + place]),
    )


def degrid_grid(own_list, own_count, kernel_mat, kernel_adj, gathered, own_data):
    blocks, chans, parts, rows, width = gathered.shape
    slots = own_list.shape[0]
    group = 4
    out_rows, in_rows = kernel_mat.shape
    inner = tile_width
    flops = 4 * out_rows * in_rows * inner * chans * slots
    return pl.pallas_call(
        degrid_body,
        grid_spec=pltpu.PrefetchScalarGridSpec(
            num_scalar_prefetch=2,
            grid=(chans, slots // group),
            in_specs=[
                pl.BlockSpec((out_rows, in_rows), lambda c, s, lst, cnt: (0, 0)),
                pl.BlockSpec((in_rows, out_rows), lambda c, s, lst, cnt: (0, 0)),
            ]
            + [tile_spec(blocks, parts, rows, inner, group, place) for place in range(group)]
            + [
                pl.BlockSpec(
                    (None, parts, group, out_rows // parts, inner),
                    lambda c, s, lst, cnt: (c, 0, s, 0, 0),
                ),
            ],
            out_specs=pl.BlockSpec((None, group, in_rows, inner), lambda c, s, lst, cnt: (c, s, 0, 0)),
        ),
        out_shape=jax.ShapeDtypeStruct((chans, slots, in_rows, inner), jnp.bfloat16),
        cost_estimate=pl.CostEstimate(
            flops=flops, bytes_accessed=2 * chans * slots * (out_rows + 2 * in_rows) * inner,
            transcendentals=0,
        ),
    )(own_list, own_count, kernel_mat, kernel_adj, *([gathered] * group), own_data)


def per_device(image, wavelet_dual, weights, kernels, vis_data, tile_list, tile_count):
    panel_rows, chan_count, grid_width = image.shape
    inner = tile_width
    outer = grid_width // inner
    unit_scale = 1.0 / math.sqrt(grid_width)
    bf = jnp.bfloat16
    f32 = jnp.float32
    own_list = tile_list[0, 0]
    own_count = tile_count[0, 0]
    slots_count = own_list.shape[0]
    image_rows = image.reshape(panel_rows * chan_count, grid_width)
    grid_re, grid_im = fourier_rows(image_rows, jnp.zeros_like(image_rows), -1.0)
    grid_panel = (
        jnp.stack([grid_re, grid_im], axis=1)
        .reshape(panel_rows, chan_count, 2, grid_width)
        .astype(bf)
    )
    panel_t = jnp.transpose(grid_panel, (1, 2, 0, 3))
    gathered = lax.all_gather(panel_t, "vis", axis=0)
    blocks = gathered.shape[0]
    stacked = kernel_blocks(kernels[0, 0])
    out_rows, vis_rows = stacked.shape[0] * stacked.shape[1], stacked.shape[2] * blocks * panel_rows
    kernel_mat = jnp.transpose(
        stacked.reshape(2, -1, 2, blocks, panel_rows), (0, 1, 3, 2, 4)
    ).reshape(out_rows, vis_rows)
    kernel_adj = jnp.transpose(kernel_mat)
    own_data = vis_data[0, 0]
    partial = degrid_grid(own_list, own_count.reshape(1), kernel_mat, kernel_adj, gathered, own_data)
    partial = partial.reshape(chan_count, slots_count, blocks, 2, panel_rows, inner)
    inner_index = jnp.arange(inner, dtype=jnp.int32)
    outer_index = jnp.arange(outer, dtype=jnp.int32)
    cos_in, sin_in = angle_table(inner_index, inner_index, inner)
    cos_tw, sin_tw = angle_table(outer_index, inner_index, grid_width)
    cos_sel, sin_sel = angle_table(outer_index, own_list, outer)
    tw_c = cos_tw[None, :, None, None, :]
    tw_s = sin_tw[None, :, None, None, :]
    inv_c = jnp.transpose(cos_sel).astype(bf)
    inv_s = jnp.transpose(sin_sel).astype(bf)
    inverse_mat = jnp.stack([jnp.stack([inv_c, -inv_s]), jnp.stack([inv_s, inv_c])])
    back = jnp.einsum(
        "jisa,csvirk->jvacrk", inverse_mat, partial, preferred_element_type=f32
    ).astype(bf)
    back_re = back[0].astype(f32)
    back_im = back[1].astype(f32)
    turned_re = (back_re * tw_c - back_im * tw_s).astype(bf)
    turned_im = (back_re * tw_s + back_im * tw_c).astype(bf)
    out_c = (cos_in * unit_scale).astype(bf)
    out_s = (sin_in * unit_scale).astype(bf)
    rows_part = jnp.einsum("vacrk,kb->vacrb", turned_re, out_c, preferred_element_type=f32) - jnp.einsum(
        "vacrk,kb->vacrb", turned_im, out_s, preferred_element_type=f32
    )
    rows_sum = lax.psum_scatter(rows_part.astype(bf), "vis", scatter_dimension=0, tiled=True)
    gradient = (
        jnp.transpose(rows_sum[0].astype(f32), (2, 1, 3, 0))
        .reshape(panel_rows, chan_count, grid_width)
    )
    upper_rim = shifted(
        wavelet_dual[panel_rows - 3 :].astype(jnp.bfloat16), ("facet", "vis"), 1
    ).astype(jnp.float32)
    padded_dual = jnp.concatenate([upper_rim, wavelet_dual], axis=0)
    synthesized = jnp.zeros_like(wavelet_dual)
    for offset in range(4):
        synthesized = (
            synthesized + high_taps[offset] * padded_dual[3 - offset : 3 - offset + panel_rows]
        )
    image_next = jnp.maximum(image - primal_step * (gradient + synthesized), 0.0)
    extrap = 2.0 * image_next - image
    lower_rim = shifted(for_sending(extrap[:3]), ("facet", "vis"), -1)
    padded_next = jnp.concatenate([extrap, lower_rim], axis=0)
    detail = jnp.zeros_like(extrap)
    for offset in range(4):
        detail = detail + high_taps[offset] * padded_next[offset : offset + panel_rows]
    update = wavelet_dual + dual_step * detail
    own_energy = jnp.sum(update * update, axis=1)
    other_energy = lax.ppermute(own_energy.astype(bf), "spec", [(0, 1), (1, 0)])
    energy = own_energy + other_energy.astype(f32)
    dual_next = update * weights[:, None, :] / jnp.maximum(weights, jnp.sqrt(energy))[:, None, :]
    return (image_next, dual_next)


def solution(mesh):
    return jax.shard_map(
        per_device,
        mesh=mesh,
        in_specs=(
            P(("facet", "vis"), "spec", None),
            P(("facet", "vis"), "spec", None),
            P(("facet", "vis"), None),
            P("facet", "vis", None, None, None),
            P("facet", "vis", "spec", None, None, None, None),
            P("facet", "vis", None),
            P("facet", "vis"),
        ),
        out_specs=(P(("facet", "vis"), "spec", None), P(("facet", "vis"), "spec", None)),
        check_vma=False,
    )
```
